32 devices in a mesh: dp: 8 (over z, y), feat: 4 (over x, core).
Axes of the slice: x: 2, y: 2, z: 4, core: 2. Of those that a mesh axis runs over, the one named last changes fastest.
Arguments:
- activations: bfloat16 [16384, 2048], P('feat', 'dp'), may hold values from -6 to 6
- cotangent: bfloat16 [16384, 2048], P('feat', 'dp'), may hold values from -6 to 6
- r_mix: bfloat16 [64, 256, 256], P('feat', 'dp'), may hold values from -0.375 to 0.375
- l_mix: bfloat16 [256, 4096], P('feat', 'dp'), may hold values from -0.75 to 0.75
Outputs:
- grad_x: bfloat16 [16384, 2048], P('feat', 'dp')
- grad_r: float32 [64, 256, 256], P('feat', 'dp')
- grad_l: float32 [256, 4096], P('feat', 'dp')
The draws below stay inside these ranges and needn't reach their ends.
All inputs are finite; a program needn't handle non-finite values.
Results may differ from the reference program's by a relative error of at most 0.0055.
Values may be sent and summed in bfloat16 or wider, within the bound.
No kernel may reach another device: no remote copies, remote signals or barrier semaphores. Data moves between devices by JAX's collectives and lax.ppermute only.
A program may use at most 64 MiB of HBM per device.

```python
import jax
import jax.numpy as jnp
from jax import lax

BLOCKS = 64
WIDTH = 256
TOK_DEV = 256
HIDDEN_SIZE = 16384
TOKENS = 2048


def steps_of(stream_key, dims, cuts, low, largest):
    level = 1.0
    for axis_at, parts in cuts:
        draws = jax.random.uniform(jax.random.fold_in(jax.random.fold_in(stream_key, 6), axis_at), (parts,), jnp.float32, low / len(cuts), largest / len(cuts))
        level = level * jnp.repeat(jnp.exp(draws), dims[axis_at] // parts).reshape((-1,) + (1,) * (len(dims) - 1 - axis_at))
    return level


def centred(rng, dims, deviation, most, split=(), dtype=jnp.bfloat16):
    level = steps_of(rng, dims, split, -0.22, 0.18) if split else 1.0
    values = jax.random.normal(rng, dims, jnp.float32) * deviation * level
    return jnp.minimum(jnp.maximum(values, -most), most).astype(dtype)


def setup_inputs(seed: int = 0) -> dict:
    key_list = jax.random.split(jax.random.key(seed), 5)
    activations = centred(key_list[0], (HIDDEN_SIZE, TOKENS), 1.0, 6.0, ((0, 4), (1, 8)))
    cotangent = centred(key_list[1], (HIDDEN_SIZE, TOKENS), 1.0, 6.0, ((0, 4), (1, 8)))
    r_mix = centred(key_list[2], (BLOCKS, WIDTH, WIDTH), WIDTH ** -0.5, 0.375, ((0, 4), (1, 8)))
    l_mix = centred(key_list[3], (WIDTH, BLOCKS * BLOCKS), BLOCKS ** -0.5, 0.75, ((0, 4), (1, 8)))
    return {"activations": activations, "cotangent": cotangent, "r_mix": r_mix, "l_mix": l_mix}


def gelu_tanh(values):
    return jax.nn.gelu(values, approximate=True)

def tile_pass(x_tile, g_tile, r_mix, l_mix):
    count = x_tile.shape[1]
    x_blocks = x_tile.reshape(BLOCKS, WIDTH, count).astype(jnp.float32)
    g_blocks = g_tile.reshape(BLOCKS, WIDTH, count).astype(jnp.float32)
    r_float = r_mix.astype(jnp.float32)
    l_blocks = l_mix.reshape(WIDTH, BLOCKS, BLOCKS).astype(jnp.float32)
    mixed = jnp.einsum('bit,bio->bot', x_blocks, r_float).astype(jnp.bfloat16)
    pre_act = jnp.einsum('bst,sbc->cst', mixed.astype(jnp.float32), l_blocks)
    _, pullback = jax.vjp(gelu_tanh, pre_act)
    slope = pullback(g_blocks)[0].astype(jnp.bfloat16)
    back_cols = jnp.einsum('cst,sbc->bst', slope.astype(jnp.float32), l_blocks).astype(jnp.bfloat16)
    grad_l_part = jnp.einsum('bst,cst->sbc', mixed.astype(jnp.float32), slope.astype(jnp.float32))
    back_float = back_cols.astype(jnp.float32)
    grad_x_tile = (g_blocks + jnp.einsum('bot,bio->bit', back_float, r_float)).astype(jnp.bfloat16)
    grad_r_part = jnp.einsum('bit,bot->bio', x_blocks, back_float)
    return (grad_x_tile.reshape(HIDDEN_SIZE, count), grad_r_part, grad_l_part)

def reference(activations, cotangent, r_mix, l_mix):
    tiles = TOKENS // TOK_DEV
    x_tiles = jnp.transpose(activations.reshape(HIDDEN_SIZE, tiles, TOK_DEV), (1, 0, 2))
    g_tiles = jnp.transpose(cotangent.reshape(HIDDEN_SIZE, tiles, TOK_DEV), (1, 0, 2))

    def step(carry, pair):
        grad_x_tile, grad_r_part, grad_l_part = tile_pass(pair[0], pair[1], r_mix, l_mix)
        return ((carry[0] + grad_r_part, carry[1] + grad_l_part), grad_x_tile)
    start = (jnp.zeros((BLOCKS, WIDTH, WIDTH), jnp.float32), jnp.zeros((WIDTH, BLOCKS, BLOCKS), jnp.float32))
    (grad_r_sum, grad_l_sum), grad_x_tiles = lax.scan(step, start, (x_tiles, g_tiles))
    grad_x = jnp.transpose(grad_x_tiles, (1, 0, 2)).reshape(HIDDEN_SIZE, TOKENS)
    factor = 1.0 / jnp.sqrt(jnp.float32(TOKENS))
    grad_r = grad_r_sum * factor
    grad_l = grad_l_sum.reshape(WIDTH, BLOCKS * BLOCKS) * factor
    return (grad_x, grad_r, grad_l)
```

```python
import math

import jax
import jax.numpy as jnp
from jax import lax
from jax.sharding import PartitionSpec as P

BLOCKS = 64
WIDTH = 256


def gelu_tanh(values):
    return jax.nn.gelu(values, approximate=True)


def slope_of(pre_act, upstream):
    _, pullback = jax.vjp(gelu_tanh, pre_act)
    return pullback(upstream.astype(jnp.float32))[0].astype(jnp.bfloat16)


def body(activations, cotangent, r_mix, l_mix):
    tok_count = activations.shape[1]
    local_blocks = activations.shape[0] // WIDTH
    grad_scale = 1.0 / math.sqrt(tok_count * lax.axis_size("dp"))
    x_blocks = activations.reshape(local_blocks, WIDTH, tok_count)
    g_blocks = cotangent.reshape(local_blocks, WIDTH, tok_count)
    g_cols = lax.all_to_all(g_blocks, "feat", split_axis=1, concat_axis=0, tiled=True)
    r_lead = jnp.transpose(r_mix, (1, 0, 2))
    r_whole = lax.all_gather(r_lead, "dp", axis=0, tiled=True)
    local_cols = l_mix.shape[0]
    l_lead = jnp.transpose(l_mix.reshape(local_cols, -1, BLOCKS), (1, 0, 2))
    l_blocks = lax.all_gather(l_lead, "dp", axis=0, tiled=True)
    mixed_rows = jnp.einsum(
        "bit,ibo->bot", x_blocks, r_whole, preferred_element_type=jnp.float32
    ).astype(jnp.bfloat16)
    columns = lax.all_to_all(mixed_rows, "feat", split_axis=1, concat_axis=0, tiled=True)
    pre_act = jnp.einsum("bst,bsc->cst", columns, l_blocks, preferred_element_type=jnp.float32)
    slope_cols = slope_of(pre_act, g_cols)
    back_cols = jnp.einsum(
        "cst,bsc->bst", slope_cols, l_blocks, preferred_element_type=jnp.float32
    ).astype(jnp.bfloat16)
    l_term = jnp.einsum("bst,cst->bsc", columns, slope_cols, preferred_element_type=jnp.float32)
    l_term = l_term * grad_scale
    grad_l = lax.psum_scatter(l_term, "dp", scatter_dimension=0, tiled=True)
    grad_l = jnp.transpose(grad_l, (1, 0, 2)).reshape(local_cols, -1)
    back_rows = lax.all_to_all(back_cols, "feat", split_axis=0, concat_axis=1, tiled=True)
    through_r = jnp.einsum("bot,ibo->bit", back_rows, r_whole, preferred_element_type=jnp.float32)
    grad_x = (
        (g_blocks.astype(jnp.float32) + through_r)
        .astype(jnp.bfloat16)
        .reshape(local_blocks * WIDTH, tok_count)
    )
    r_term = (
        jnp.einsum("bit,bot->ibo", x_blocks, back_rows, preferred_element_type=jnp.float32)
        * grad_scale
    )
    grad_r = lax.psum_scatter(r_term, "dp", scatter_dimension=0, tiled=True)
    grad_r = jnp.transpose(grad_r, (1, 0, 2))
    return (grad_x, grad_r, grad_l)


def solution(mesh):
    placed = (P("feat", "dp"), P("feat", "dp"), P("feat", "dp", None), P("feat", "dp"))
    return jax.shard_map(
        body,
        mesh=mesh,
        in_specs=placed,
        out_specs=(P("feat", "dp"), P("feat", "dp", None), P("feat", "dp")),
        check_vma=False,
    )
```

```python
import math

import jax
import jax.numpy as jnp
import numpy as np
from jax import lax
from jax.sharding import PartitionSpec as P

BLOCKS = 64
WIDTH = 256


def gelu_tanh(values):
    return jax.nn.gelu(values, approximate=True)


def slope_of(pre_act, upstream):
    _, pullback = jax.vjp(gelu_tanh, pre_act)
    return pullback(upstream.astype(jnp.float32))[0].astype(jnp.bfloat16)


def ring_of(mesh):
    row = mesh.devices[(slice(None),) + (0,) * (mesh.devices.ndim - 1)]
    size = len(row)
    try:
        spots = [tuple(d.coords) for d in row]
    except AttributeError:
        return list(range(size))
    near = [
        [j for j in range(size) if sum(abs(a - b) for a, b in zip(spots[i], spots[j])) == 1]
        for i in range(size)
    ]
    path, seen, budget = [0], {0}, [20000]

    def grow():
        budget[0] -= 1
        if budget[0] < 0:
            return False
        if len(path) == size:
            return 0 in near[path[-1]] or size <= 2
        here = path[-1]
        for nxt in sorted(near[here], key=lambda j: len([k for k in near[j] if k not in seen])):
            if nxt in seen:
                continue
            path.append(nxt)
            seen.add(nxt)
            if grow():
                return True
            path.pop()
            seen.discard(nxt)
        return False

    return list(path) if grow() else list(range(size))


def ring_reduce_scatter(parts, ring):
    n = len(ring)
    order = jnp.asarray(np.array(ring, np.int32))
    place = jnp.asarray(np.argsort(np.array(ring)).astype(np.int32))
    here = place[lax.axis_index("dp")]
    half = parts.shape[1] // 2
    halves = (parts[:, :half], parts[:, half:])
    forward = [(ring[p], ring[(p + 1) % n]) for p in range(n)]
    backward = [(ring[p], ring[(p - 1) % n]) for p in range(n)]
    totals = []
    for way, pairs, src in ((1, forward, halves[0]), (-1, backward, halves[1])):
        acc = None
        for step in range(n):
            owner = order[(here - way * (1 + step)) % n]
            mine = lax.dynamic_index_in_dim(src, owner, axis=0, keepdims=False)
            acc = mine if acc is None else acc + mine
            if step < n - 1:
                acc = lax.ppermute(acc, "dp", pairs)
        totals.append(acc)
    return jnp.concatenate(totals, axis=0)


def body(ring, activations, cotangent, r_mix, l_mix):
    tok_count = activations.shape[1]
    local_blocks = activations.shape[0] // WIDTH
    n_dp = lax.axis_size("dp")
    grad_scale = 1.0 / math.sqrt(tok_count * n_dp)
    x_blocks = activations.reshape(local_blocks, WIDTH, tok_count)
    g_blocks = cotangent.reshape(local_blocks, WIDTH, tok_count)
    g_cols = lax.all_to_all(g_blocks, "feat", split_axis=1, concat_axis=0, tiled=True)
    local_cols = l_mix.shape[0]
    rows_r = r_mix.shape[1]
    r_flat = r_mix.reshape(1, -1)
    packed = jnp.concatenate([r_flat, l_mix.reshape(1, -1)], axis=1)
    packed = lax.all_gather(packed, "dp", axis=0, tiled=True)
    r_size = r_flat.shape[1]
    r_whole = packed[:, :r_size].reshape(n_dp, local_blocks, rows_r, WIDTH)
    r_whole = jnp.transpose(r_whole, (1, 0, 2, 3)).reshape(local_blocks, n_dp * rows_r, WIDTH)
    l_whole = packed[:, r_size:].reshape(n_dp, local_cols, -1, BLOCKS)
    l_blocks = jnp.transpose(l_whole, (0, 2, 1, 3)).reshape(-1, local_cols, BLOCKS)
    mixed_rows = jnp.einsum(
        "bit,bio->bot", x_blocks, r_whole, preferred_element_type=jnp.float32
    ).astype(jnp.bfloat16)
    columns = lax.all_to_all(mixed_rows, "feat", split_axis=1, concat_axis=0, tiled=True)
    pre_act = jnp.einsum("bst,bsc->cst", columns, l_blocks, preferred_element_type=jnp.float32)
    slope_cols = slope_of(pre_act, g_cols)
    back_cols = jnp.einsum(
        "cst,bsc->sbt", slope_cols, l_blocks, preferred_element_type=jnp.float32
    ).astype(jnp.bfloat16)
    l_term = jnp.einsum("bst,cst->bsc", columns, slope_cols, preferred_element_type=jnp.float32)
    l_term = (l_term * grad_scale).reshape(n_dp, -1, local_cols, BLOCKS)
    grad_l = ring_reduce_scatter(l_term, ring)
    grad_l = jnp.transpose(grad_l, (1, 0, 2)).reshape(local_cols, -1)
    back_rows = lax.all_to_all(back_cols, "feat", split_axis=1, concat_axis=0, tiled=True)
    through_r = jnp.einsum("obt,bio->bit", back_rows, r_whole, preferred_element_type=jnp.float32)
    grad_x = (
        (g_blocks.astype(jnp.float32) + through_r)
        .astype(jnp.bfloat16)
        .reshape(local_blocks * WIDTH, tok_count)
    )
    r_term = (
        jnp.einsum("bit,obt->ibo", x_blocks, back_rows, preferred_element_type=jnp.float32)
        * grad_scale
    ).reshape(n_dp, rows_r, local_blocks, WIDTH)
    grad_r = ring_reduce_scatter(r_term, ring)
    grad_r = jnp.transpose(grad_r, (1, 0, 2))
    return (grad_x, grad_r, grad_l)


def solution(mesh):
    ring = ring_of(mesh)
    placed = (P("feat", "dp"), P("feat", "dp"), P("feat", "dp", None), P("feat", "dp"))
    return jax.shard_map(
        lambda *args: body(ring, *args),
        mesh=mesh,
        in_specs=placed,
        out_specs=(P("feat", "dp"), P("feat", "dp", None), P("feat", "dp")),
        check_vma=False,
    )
```

```python
import math

import jax
import jax.numpy as jnp
import numpy as np
from jax import lax
from jax.sharding import PartitionSpec as P

BLOCKS = 64
WIDTH = 256


def gelu_tanh(values):
    return jax.nn.gelu(values, approximate=True)


def slope_of(pre_act, upstream):
    _, pullback = jax.vjp(gelu_tanh, pre_act)
    return pullback(upstream.astype(jnp.float32))[0].astype(jnp.bfloat16)


def ring_of(mesh):
    row = mesh.devices[(slice(None),) + (0,) * (mesh.devices.ndim - 1)]
    size = len(row)
    try:
        spots = [tuple(d.coords) for d in row]
    except AttributeError:
        return list(range(size))
    near = [
        [j for j in range(size) if sum(abs(a - b) for a, b in zip(spots[i], spots[j])) == 1]
        for i in range(size)
    ]
    path, seen, budget = [0], {0}, [20000]

    def grow():
        budget[0] -= 1
        if budget[0] < 0:
            return False
        if len(path) == size:
            return 0 in near[path[-1]] or size <= 2
        here = path[-1]
        for nxt in sorted(near[here], key=lambda j: len([k for k in near[j] if k not in seen])):
            if nxt in seen:
                continue
            path.append(nxt)
            seen.add(nxt)
            if grow():
                return True
            path.pop()
            seen.discard(nxt)
        return False

    return list(path) if grow() else list(range(size))


def ring_reduce_scatter(parts, ring):
    n = len(ring)
    order = jnp.asarray(np.array(ring, np.int32))
    place = jnp.asarray(np.argsort(np.array(ring)).astype(np.int32))
    here = place[lax.axis_index("dp")]
    half = parts.shape[1] // 2
    halves = (parts[:, :half], parts[:, half:])
    forward = [(ring[p], ring[(p + 1) % n]) for p in range(n)]
    backward = [(ring[p], ring[(p - 1) % n]) for p in range(n)]
    totals = []
    for way, pairs, src in ((1, forward, halves[0]), (-1, backward, halves[1])):
        acc = None
        for step in range(n):
            owner = order[(here - way * (1 + step)) % n]
            mine = lax.dynamic_index_in_dim(src, owner, axis=0, keepdims=False)
            acc = mine if acc is None else acc + mine
            if step < n - 1:
                acc = lax.ppermute(acc, "dp", pairs)
        totals.append(acc)
    return jnp.concatenate(totals, axis=0)


def body(ring, activations, cotangent, r_mix, l_mix):
    tok_count = activations.shape[1]
    local_blocks = activations.shape[0] // WIDTH
    n_dp = lax.axis_size("dp")
    grad_scale = 1.0 / math.sqrt(tok_count * n_dp)
    x_blocks = activations.reshape(local_blocks, WIDTH, tok_count)
    g_blocks = cotangent.reshape(local_blocks, WIDTH, tok_count)
    g_cols = lax.all_to_all(g_blocks, "feat", split_axis=1, concat_axis=0, tiled=True)
    local_cols = l_mix.shape[0]
    rows_r = r_mix.shape[1]
    r_lead = jnp.transpose(r_mix, (1, 0, 2)).reshape(-1, WIDTH)
    l_lead = jnp.transpose(l_mix.reshape(local_cols, -1, BLOCKS), (1, 0, 2)).reshape(-1, WIDTH)
    r_size = r_lead.shape[0]
    packed = jnp.concatenate([r_lead, l_lead], axis=0)[None]
    packed = lax.all_gather(packed, "dp", axis=0, tiled=True)
    r_whole = packed[:, :r_size].reshape(n_dp * rows_r, local_blocks, WIDTH)
    l_blocks = packed[:, r_size:].reshape(-1, local_cols, BLOCKS)
    mixed_rows = jnp.einsum(
        "bit,ibo->bot", x_blocks, r_whole, preferred_element_type=jnp.float32
    ).astype(jnp.bfloat16)
    columns = lax.all_to_all(mixed_rows, "feat", split_axis=1, concat_axis=0, tiled=True)
    pre_act = jnp.einsum("bst,bsc->cst", columns, l_blocks, preferred_element_type=jnp.float32)
    slope_cols = slope_of(pre_act, g_cols)
    back_cols = jnp.einsum(
        "cst,bsc->sbt", slope_cols, l_blocks, preferred_element_type=jnp.float32
    ).astype(jnp.bfloat16)
    l_term = jnp.einsum("bst,cst->bsc", columns, slope_cols, preferred_element_type=jnp.float32)
    l_term = (l_term * grad_scale).reshape(n_dp, -1, local_cols, BLOCKS)
    grad_l = ring_reduce_scatter(l_term, ring)
    grad_l = jnp.transpose(grad_l, (1, 0, 2)).reshape(local_cols, -1)
    back_rows = lax.all_to_all(back_cols, "feat", split_axis=1, concat_axis=0, tiled=True)
    through_r = jnp.einsum("obt,ibo->bit", back_rows, r_whole, preferred_element_type=jnp.float32)
    grad_x = (
        (g_blocks.astype(jnp.float32) + through_r)
        .astype(jnp.bfloat16)
        .reshape(local_blocks * WIDTH, tok_count)
    )
    r_term = (
        jnp.einsum("bit,obt->ibo", x_blocks, back_rows, preferred_element_type=jnp.float32)
        * grad_scale
    ).reshape(n_dp, rows_r, local_blocks, WIDTH)
    grad_r = ring_reduce_scatter(r_term, ring)
    grad_r = jnp.transpose(grad_r, (1, 0, 2))
    return (grad_x, grad_r, grad_l)


def solution(mesh):
    ring = ring_of(mesh)
    placed = (P("feat", "dp"), P("feat", "dp"), P("feat", "dp", None), P("feat", "dp"))
    return jax.shard_map(
        lambda *args: body(ring, *args),
        mesh=mesh,
        in_specs=placed,
        out_specs=(P("feat", "dp"), P("feat", "dp", None), P("feat", "dp")),
        check_vma=False,
    )
```

```python
import math

import jax
import jax.numpy as jnp
import numpy as np
from jax import lax
from jax.sharding import PartitionSpec as P

BLOCKS = 64
WIDTH = 256


def gelu_tanh(values):
    return jax.nn.gelu(values, approximate=True)


def slope_of(pre_act, upstream):
    _, pullback = jax.vjp(gelu_tanh, pre_act)
    return pullback(upstream.astype(jnp.float32))[0].astype(jnp.bfloat16)


def ring_of(mesh):
    row = mesh.devices[(slice(None),) + (0,) * (mesh.devices.ndim - 1)]
    size = len(row)
    try:
        spots = [tuple(d.coords) for d in row]
    except AttributeError:
        return list(range(size))
    near = [
        [j for j in range(size) if sum(abs(a - b) for a, b in zip(spots[i], spots[j])) == 1]
        for i in range(size)
    ]
    path, seen, budget = [0], {0}, [20000]

    def grow():
        budget[0] -= 1
        if budget[0] < 0:
            return False
        if len(path) == size:
            return 0 in near[path[-1]] or size <= 2
        here = path[-1]
        for nxt in sorted(near[here], key=lambda j: len([k for k in near[j] if k not in seen])):
            if nxt in seen:
                continue
            path.append(nxt)
            seen.add(nxt)
            if grow():
                return True
            path.pop()
            seen.discard(nxt)
        return False

    return list(path) if grow() else list(range(size))


def ring_reduce_scatter(parts, ring):
    n = len(ring)
    order = jnp.asarray(np.array(ring, np.int32))
    place = jnp.asarray(np.argsort(np.array(ring)).astype(np.int32))
    here = place[lax.axis_index("dp")]
    half = parts.shape[1] // 2
    halves = (parts[:, :half], parts[:, half:])
    forward = [(ring[p], ring[(p + 1) % n]) for p in range(n)]
    backward = [(ring[p], ring[(p - 1) % n]) for p in range(n)]
    totals = []
    for way, pairs, src in ((1, forward, halves[0]), (-1, backward, halves[1])):
        acc = None
        for step in range(n):
            owner = order[(here - way * (1 + step)) % n]
            mine = lax.dynamic_index_in_dim(src, owner, axis=0, keepdims=False)
            acc = mine if acc is None else acc + mine
            if step < n - 1:
                acc = lax.ppermute(acc, "dp", pairs)
        totals.append(acc)
    return jnp.concatenate(totals, axis=0)


def body(ring, activations, cotangent, r_mix, l_mix):
    tok_count = activations.shape[1]
    local_blocks = activations.shape[0] // WIDTH
    n_dp = lax.axis_size("dp")
    grad_scale = 1.0 / math.sqrt(tok_count * n_dp)
    x_blocks = activations.reshape(local_blocks, WIDTH, tok_count)
    g_blocks = cotangent.reshape(local_blocks, WIDTH, tok_count)
    n_feat = lax.axis_size("feat")
    g_out = jnp.transpose(g_blocks.reshape(local_blocks, n_feat, -1, tok_count), (1, 0, 2, 3))
    g_cols = lax.all_to_all(g_out, "feat", split_axis=0, concat_axis=0, tiled=True)
    g_cols = g_cols.reshape(-1, WIDTH // n_feat, tok_count)
    local_cols = l_mix.shape[0]
    rows_r = r_mix.shape[1]
    r_lead = jnp.transpose(r_mix, (1, 0, 2)).reshape(-1, WIDTH)
    l_lead = jnp.transpose(l_mix.reshape(local_cols, -1, BLOCKS), (1, 0, 2)).reshape(-1, WIDTH)
    r_size = r_lead.shape[0]
    packed = jnp.concatenate([r_lead, l_lead], axis=0)[None]
    packed = lax.all_gather(packed, "dp", axis=0, tiled=True)
    r_whole = packed[:, :r_size].reshape(n_dp * rows_r, local_blocks, WIDTH)
    l_blocks = packed[:, r_size:].reshape(-1, local_cols, BLOCKS)
    r_split = r_whole.reshape(n_dp * rows_r, local_blocks, n_feat, -1)
    mixed_out = jnp.einsum(
        "bit,ibqs->qbst", x_blocks, r_split, preferred_element_type=jnp.float32
    ).astype(jnp.bfloat16)
    columns = lax.all_to_all(mixed_out, "feat", split_axis=0, concat_axis=0, tiled=True)
    columns = columns.reshape(-1, WIDTH // n_feat, tok_count)
    pre_act = jnp.einsum("bst,bsc->cst", columns, l_blocks, preferred_element_type=jnp.float32)
    slope_cols = slope_of(pre_act, g_cols)
    back_cols = jnp.einsum(
        "cst,bsc->bst", slope_cols, l_blocks, preferred_element_type=jnp.float32
    ).astype(jnp.bfloat16)
    l_term = jnp.einsum("bst,cst->bsc", columns, slope_cols, preferred_element_type=jnp.float32)
    l_term = (l_term * grad_scale).reshape(n_dp, -1, local_cols, BLOCKS)
    grad_l = ring_reduce_scatter(l_term, ring)
    grad_l = jnp.transpose(grad_l, (1, 0, 2)).reshape(local_cols, -1)
    back_out = back_cols.reshape(n_feat, local_blocks, -1, tok_count)
    back_rows = lax.all_to_all(back_out, "feat", split_axis=0, concat_axis=0, tiled=True)
    through_r = jnp.einsum("qbst,ibqs->bit", back_rows, r_split, preferred_element_type=jnp.float32)
    grad_x = (
        (g_blocks.astype(jnp.float32) + through_r)
        .astype(jnp.bfloat16)
        .reshape(local_blocks * WIDTH, tok_count)
    )
    r_term = (
        jnp.einsum("bit,qbst->ibqs", x_blocks, back_rows, preferred_element_type=jnp.float32)
        * grad_scale
    ).reshape(n_dp, rows_r, local_blocks, WIDTH)
    grad_r = ring_reduce_scatter(r_term, ring)
    grad_r = jnp.transpose(grad_r, (1, 0, 2))
    return (grad_x, grad_r, grad_l)


def solution(mesh):
    ring = ring_of(mesh)
    placed = (P("feat", "dp"), P("feat", "dp"), P("feat", "dp", None), P("feat", "dp"))
    return jax.shard_map(
        lambda *args: body(ring, *args),
        mesh=mesh,
        in_specs=placed,
        out_specs=(P("feat", "dp"), P("feat", "dp", None), P("feat", "dp")),
        check_vma=False,
    )
```

```python
import math

import jax
import jax.numpy as jnp
import numpy as np
from jax import lax
from jax.sharding import PartitionSpec as P

BLOCKS = 64
WIDTH = 256


def gelu_tanh(values):
    return jax.nn.gelu(values, approximate=True)


def slope_of(pre_act, upstream):
    _, pullback = jax.vjp(gelu_tanh, pre_act)
    return pullback(upstream.astype(jnp.float32))[0].astype(jnp.bfloat16)


def ring_of(mesh):
    row = mesh.devices[(slice(None),) + (0,) * (mesh.devices.ndim - 1)]
    size = len(row)
    try:
        spots = [tuple(d.coords) for d in row]
    except AttributeError:
        return list(range(size))
    near = [
        [j for j in range(size) if sum(abs(a - b) for a, b in zip(spots[i], spots[j])) == 1]
        for i in range(size)
    ]
    path, seen, budget = [0], {0}, [20000]

    def grow():
        budget[0] -= 1
        if budget[0] < 0:
            return False
        if len(path) == size:
            return 0 in near[path[-1]] or size <= 2
        here = path[-1]
        for nxt in sorted(near[here], key=lambda j: len([k for k in near[j] if k not in seen])):
            if nxt in seen:
                continue
            path.append(nxt)
            seen.add(nxt)
            if grow():
                return True
            path.pop()
            seen.discard(nxt)
        return False

    return list(path) if grow() else list(range(size))


def ring_reduce_scatter(parts, ring):
    n = len(ring)
    order = jnp.asarray(np.array(ring, np.int32))
    place = jnp.asarray(np.argsort(np.array(ring)).astype(np.int32))
    here = place[lax.axis_index("dp")]
    half = parts.shape[1] // 2
    halves = (parts[:, :half], parts[:, half:])
    forward = [(ring[p], ring[(p + 1) % n]) for p in range(n)]
    backward = [(ring[p], ring[(p - 1) % n]) for p in range(n)]
    totals = []
    for way, pairs, src in ((1, forward, halves[0]), (-1, backward, halves[1])):
        acc = None
        for step in range(n):
            owner = order[(here - way * (1 + step)) % n]
            mine = lax.dynamic_index_in_dim(src, owner, axis=0, keepdims=False)
            acc = mine if acc is None else acc + mine
            if step < n - 1:
                acc = lax.ppermute(acc, "dp", pairs)
        totals.append(acc)
    return jnp.concatenate(totals, axis=0)


def ring_all_gather(piece, ring):
    n = len(ring)
    order = jnp.asarray(np.array(ring, np.int32))
    place = jnp.asarray(np.argsort(np.array(ring)).astype(np.int32))
    me = lax.axis_index("dp")
    here = place[me]
    half = piece.shape[0] // 2
    forward = [(ring[p], ring[(p + 1) % n]) for p in range(n)]
    backward = [(ring[p], ring[(p - 1) % n]) for p in range(n)]
    outs = []
    for way, pairs, src in ((1, forward, piece[:half]), (-1, backward, piece[half:])):
        held = lax.dynamic_update_index_in_dim(jnp.zeros((n,) + src.shape, src.dtype), src, me, 0)
        cur = src
        for step in range(n - 1):
            cur = lax.ppermute(cur, "dp", pairs)
            owner = order[(here - way * (1 + step)) % n]
            held = lax.dynamic_update_index_in_dim(held, cur, owner, 0)
        outs.append(held)
    return jnp.concatenate(outs, axis=1)


def body(ring, activations, cotangent, r_mix, l_mix):
    tok_count = activations.shape[1]
    local_blocks = activations.shape[0] // WIDTH
    n_dp = lax.axis_size("dp")
    grad_scale = 1.0 / math.sqrt(tok_count * n_dp)
    x_blocks = activations.reshape(local_blocks, WIDTH, tok_count)
    g_blocks = cotangent.reshape(local_blocks, WIDTH, tok_count)
    g_cols = lax.all_to_all(g_blocks, "feat", split_axis=1, concat_axis=0, tiled=True)
    local_cols = l_mix.shape[0]
    rows_r = r_mix.shape[1]
    r_lead = jnp.transpose(r_mix, (1, 0, 2)).reshape(-1, WIDTH)
    l_lead = jnp.transpose(l_mix.reshape(local_cols, -1, BLOCKS), (1, 0, 2)).reshape(-1, WIDTH)
    r_size = r_lead.shape[0]
    packed = jnp.concatenate([r_lead, l_lead], axis=0)
    packed = ring_all_gather(packed, ring)
    r_whole = packed[:, :r_size].reshape(n_dp * rows_r, local_blocks, WIDTH)
    l_blocks = packed[:, r_size:].reshape(-1, local_cols, BLOCKS)
    mixed_rows = jnp.einsum(
        "bit,ibo->bot", x_blocks, r_whole, preferred_element_type=jnp.float32
    ).astype(jnp.bfloat16)
    columns = lax.all_to_all(mixed_rows, "feat", split_axis=1, concat_axis=0, tiled=True)
    pre_act = jnp.einsum("bst,bsc->cst", columns, l_blocks, preferred_element_type=jnp.float32)
    slope_cols = slope_of(pre_act, g_cols)
    back_cols = jnp.einsum(
        "cst,bsc->sbt", slope_cols, l_blocks, preferred_element_type=jnp.float32
    ).astype(jnp.bfloat16)
    l_term = jnp.einsum("bst,cst->bsc", columns, slope_cols, preferred_element_type=jnp.float32)
    l_term = (l_term * grad_scale).reshape(n_dp, -1, local_cols, BLOCKS)
    grad_l = ring_reduce_scatter(l_term, ring)
    grad_l = jnp.transpose(grad_l, (1, 0, 2)).reshape(local_cols, -1)
    back_rows = lax.all_to_all(back_cols, "feat", split_axis=1, concat_axis=0, tiled=True)
    through_r = jnp.einsum("obt,ibo->bit", back_rows, r_whole, preferred_element_type=jnp.float32)
    grad_x = (
        (g_blocks.astype(jnp.float32) + through_r)
        .astype(jnp.bfloat16)
        .reshape(local_blocks * WIDTH, tok_count)
    )
    r_term = (
        jnp.einsum("bit,obt->ibo", x_blocks, back_rows, preferred_element_type=jnp.float32)
        * grad_scale
    ).reshape(n_dp, rows_r, local_blocks, WIDTH)
    grad_r = ring_reduce_scatter(r_term, ring)
    grad_r = jnp.transpose(grad_r, (1, 0, 2))
    return (grad_x, grad_r, grad_l)


def solution(mesh):
    ring = ring_of(mesh)
    placed = (P("feat", "dp"), P("feat", "dp"), P("feat", "dp", None), P("feat", "dp"))
    return jax.shard_map(
        lambda *args: body(ring, *args),
        mesh=mesh,
        in_specs=placed,
        out_specs=(P("feat", "dp"), P("feat", "dp", None), P("feat", "dp")),
        check_vma=False,
    )
```

```python
import math

import jax
import jax.numpy as jnp
import numpy as np
from jax import lax
from jax.sharding import PartitionSpec as P

BLOCKS = 64
WIDTH = 256


def gelu_tanh(values):
    return jax.nn.gelu(values, approximate=True)


def slope_of(pre_act, upstream):
    _, pullback = jax.vjp(gelu_tanh, pre_act)
    return pullback(upstream.astype(jnp.float32))[0].astype(jnp.bfloat16)


def ring_of(mesh):
    row = mesh.devices[(slice(None),) + (0,) * (mesh.devices.ndim - 1)]
    size = len(row)
    try:
        spots = [tuple(d.coords) for d in row]
    except AttributeError:
        return list(range(size))
    near = [
        [j for j in range(size) if sum(abs(a - b) for a, b in zip(spots[i], spots[j])) == 1]
        for i in range(size)
    ]
    path, seen, budget = [0], {0}, [20000]

    def grow():
        budget[0] -= 1
        if budget[0] < 0:
            return False
        if len(path) == size:
            return 0 in near[path[-1]] or size <= 2
        here = path[-1]
        for nxt in sorted(near[here], key=lambda j: len([k for k in near[j] if k not in seen])):
            if nxt in seen:
                continue
            path.append(nxt)
            seen.add(nxt)
            if grow():
                return True
            path.pop()
            seen.discard(nxt)
        return False

    return list(path) if grow() else list(range(size))


def ring_reduce_scatter(parts, ring):
    n = len(ring)
    order = jnp.asarray(np.array(ring, np.int32))
    place = jnp.asarray(np.argsort(np.array(ring)).astype(np.int32))
    here = place[lax.axis_index("dp")]
    half = parts.shape[1] // 2
    halves = (parts[:, :half], parts[:, half:])
    forward = [(ring[p], ring[(p + 1) % n]) for p in range(n)]
    backward = [(ring[p], ring[(p - 1) % n]) for p in range(n)]
    totals = []
    for way, pairs, src in ((1, forward, halves[0]), (-1, backward, halves[1])):
        acc = None
        for step in range(n):
            owner = order[(here - way * (1 + step)) % n]
            mine = lax.dynamic_index_in_dim(src, owner, axis=0, keepdims=False)
            acc = mine if acc is None else acc + mine
            if step < n - 1:
                acc = lax.ppermute(acc, "dp", pairs)
        totals.append(acc)
    return jnp.concatenate(totals, axis=0)


def ring_all_gather(piece, ring):
    n = len(ring)
    order = jnp.asarray(np.array(ring, np.int32))
    place = jnp.asarray(np.argsort(np.array(ring)).astype(np.int32))
    me = lax.axis_index("dp")
    here = place[me]
    half = piece.shape[0] // 2
    forward = [(ring[p], ring[(p + 1) % n]) for p in range(n)]
    backward = [(ring[p], ring[(p - 1) % n]) for p in range(n)]
    outs = []
    for way, pairs, src in ((1, forward, piece[:half]), (-1, backward, piece[half:])):
        held = lax.dynamic_update_index_in_dim(jnp.zeros((n,) + src.shape, src.dtype), src, me, 0)
        cur = src
        for step in range(n - 1):
            cur = lax.ppermute(cur, "dp", pairs)
            owner = order[(here - way * (1 + step)) % n]
            held = lax.dynamic_update_index_in_dim(held, cur, owner, 0)
        outs.append(held)
    return jnp.concatenate(outs, axis=1)


def body(ring, activations, cotangent, r_mix, l_mix):
    tok_count = activations.shape[1]
    local_blocks = activations.shape[0] // WIDTH
    n_dp = lax.axis_size("dp")
    grad_scale = 1.0 / math.sqrt(tok_count * n_dp)
    x_blocks = activations.reshape(local_blocks, WIDTH, tok_count)
    g_blocks = cotangent.reshape(local_blocks, WIDTH, tok_count)
    local_cols = l_mix.shape[0]
    rows_r = r_mix.shape[1]
    r_lead = jnp.transpose(r_mix, (1, 0, 2)).reshape(-1, WIDTH)
    l_lead = jnp.transpose(l_mix.reshape(local_cols, -1, BLOCKS), (1, 0, 2)).reshape(-1, WIDTH)
    r_size = r_lead.shape[0]
    packed = jnp.concatenate([r_lead, l_lead], axis=0)
    packed = ring_all_gather(packed, ring)
    r_whole = packed[:, :r_size].reshape(n_dp * rows_r, local_blocks, WIDTH)
    l_blocks = packed[:, r_size:].reshape(-1, local_cols, BLOCKS)
    mixed_rows = jnp.einsum(
        "bit,ibo->bot", x_blocks, r_whole, preferred_element_type=jnp.float32
    ).astype(jnp.bfloat16)
    columns = lax.all_to_all(mixed_rows, "feat", split_axis=1, concat_axis=0, tiled=True)
    g_late, columns = lax.optimization_barrier((g_blocks, columns))
    g_cols = lax.all_to_all(g_late, "feat", split_axis=1, concat_axis=0, tiled=True)
    pre_act = jnp.einsum("bst,bsc->cst", columns, l_blocks, preferred_element_type=jnp.float32)
    slope_cols = slope_of(pre_act, g_cols)
    back_cols = jnp.einsum(
        "cst,bsc->sbt", slope_cols, l_blocks, preferred_element_type=jnp.float32
    ).astype(jnp.bfloat16)
    l_term = jnp.einsum("bst,cst->bsc", columns, slope_cols, preferred_element_type=jnp.float32)
    l_term = (l_term * grad_scale).reshape(n_dp, -1, local_cols, BLOCKS)
    grad_l = ring_reduce_scatter(l_term, ring)
    grad_l = jnp.transpose(grad_l, (1, 0, 2)).reshape(local_cols, -1)
    back_rows = lax.all_to_all(back_cols, "feat", split_axis=1, concat_axis=0, tiled=True)
    through_r = jnp.einsum("obt,ibo->bit", back_rows, r_whole, preferred_element_type=jnp.float32)
    grad_x = (
        (g_blocks.astype(jnp.float32) + through_r)
        .astype(jnp.bfloat16)
        .reshape(local_blocks * WIDTH, tok_count)
    )
    r_term = (
        jnp.einsum("bit,obt->ibo", x_blocks, back_rows, preferred_element_type=jnp.float32)
        * grad_scale
    ).reshape(n_dp, rows_r, local_blocks, WIDTH)
    grad_r = ring_reduce_scatter(r_term, ring)
    grad_r = jnp.transpose(grad_r, (1, 0, 2))
    return (grad_x, grad_r, grad_l)


def solution(mesh):
    ring = ring_of(mesh)
    placed = (P("feat", "dp"), P("feat", "dp"), P("feat", "dp", None), P("feat", "dp"))
    return jax.shard_map(
        lambda *args: body(ring, *args),
        mesh=mesh,
        in_specs=placed,
        out_specs=(P("feat", "dp"), P("feat", "dp", None), P("feat", "dp")),
        check_vma=False,
    )
```

```python
import math

import jax
import jax.numpy as jnp
import numpy as np
from jax import lax
from jax.sharding import PartitionSpec as P

BLOCKS = 64
WIDTH = 256


def gelu_tanh(values):
    return jax.nn.gelu(values, approximate=True)


def slope_of(pre_act, upstream):
    _, pullback = jax.vjp(gelu_tanh, pre_act)
    return pullback(upstream.astype(jnp.float32))[0].astype(jnp.bfloat16)


def ring_of(mesh):
    row = mesh.devices[(slice(None),) + (0,) * (mesh.devices.ndim - 1)]
    size = len(row)
    try:
        spots = [tuple(d.coords) for d in row]
    except AttributeError:
        return list(range(size))
    near = [
        [j for j in range(size) if sum(abs(a - b) for a, b in zip(spots[i], spots[j])) == 1]
        for i in range(size)
    ]
    path, seen, budget = [0], {0}, [20000]

    def grow():
        budget[0] -= 1
        if budget[0] < 0:
            return False
        if len(path) == size:
            return 0 in near[path[-1]] or size <= 2
        here = path[-1]
        for nxt in sorted(near[here], key=lambda j: len([k for k in near[j] if k not in seen])):
            if nxt in seen:
                continue
            path.append(nxt)
            seen.add(nxt)
            if grow():
                return True
            path.pop()
            seen.discard(nxt)
        return False

    return list(path) if grow() else list(range(size))


def ring_reduce_scatter(parts, ring):
    n = len(ring)
    order = jnp.asarray(np.array(ring, np.int32))
    place = jnp.asarray(np.argsort(np.array(ring)).astype(np.int32))
    here = place[lax.axis_index("dp")]
    half = parts.shape[1] // 2
    halves = (parts[:, :half], parts[:, half:])
    forward = [(ring[p], ring[(p + 1) % n]) for p in range(n)]
    backward = [(ring[p], ring[(p - 1) % n]) for p in range(n)]
    totals = []
    for way, pairs, src in ((1, forward, halves[0]), (-1, backward, halves[1])):
        acc = None
        for step in range(n):
            owner = order[(here - way * (1 + step)) % n]
            mine = lax.dynamic_index_in_dim(src, owner, axis=0, keepdims=False)
            acc = mine if acc is None else acc + mine
            if step < n - 1:
                acc = lax.ppermute(acc, "dp", pairs)
        totals.append(acc)
    return jnp.concatenate(totals, axis=0)


def ring_all_gather(piece, ring):
    n = len(ring)
    order = jnp.asarray(np.array(ring, np.int32))
    place = jnp.asarray(np.argsort(np.array(ring)).astype(np.int32))
    me = lax.axis_index("dp")
    here = place[me]
    forward = [(ring[p], ring[(p + 1) % n]) for p in range(n)]
    backward = [(ring[p], ring[(p - 1) % n]) for p in range(n)]
    held = lax.dynamic_update_index_in_dim(jnp.zeros((n,) + piece.shape, piece.dtype), piece, me, 0)
    ahead = n // 2
    for way, pairs, hops in ((1, forward, ahead), (-1, backward, n - 1 - ahead)):
        cur = piece
        for step in range(hops):
            cur = lax.ppermute(cur, "dp", pairs)
            owner = order[(here - way * (1 + step)) % n]
            held = lax.dynamic_update_index_in_dim(held, cur, owner, 0)
    return held

def body(ring, activations, cotangent, r_mix, l_mix):
    tok_count = activations.shape[1]
    local_blocks = activations.shape[0] // WIDTH
    n_dp = lax.axis_size("dp")
    grad_scale = 1.0 / math.sqrt(tok_count * n_dp)
    x_blocks = activations.reshape(local_blocks, WIDTH, tok_count)
    g_blocks = cotangent.reshape(local_blocks, WIDTH, tok_count)
    g_cols = lax.all_to_all(g_blocks, "feat", split_axis=1, concat_axis=0, tiled=True)
    local_cols = l_mix.shape[0]
    rows_r = r_mix.shape[1]
    r_lead = jnp.transpose(r_mix, (1, 0, 2)).reshape(-1, WIDTH)
    l_lead = jnp.transpose(l_mix.reshape(local_cols, -1, BLOCKS), (1, 0, 2)).reshape(-1, WIDTH)
    r_size = r_lead.shape[0]
    packed = jnp.concatenate([r_lead, l_lead], axis=0)
    packed = ring_all_gather(packed, ring)
    r_whole = packed[:, :r_size].reshape(n_dp * rows_r, local_blocks, WIDTH)
    l_blocks = packed[:, r_size:].reshape(-1, local_cols, BLOCKS)
    mixed_rows = jnp.einsum(
        "bit,ibo->bot", x_blocks, r_whole, preferred_element_type=jnp.float32
    ).astype(jnp.bfloat16)
    columns = lax.all_to_all(mixed_rows, "feat", split_axis=1, concat_axis=0, tiled=True)
    pre_act = jnp.einsum("bst,bsc->cst", columns, l_blocks, preferred_element_type=jnp.float32)
    slope_cols = slope_of(pre_act, g_cols)
    back_cols = jnp.einsum(
        "cst,bsc->sbt", slope_cols, l_blocks, preferred_element_type=jnp.float32
    ).astype(jnp.bfloat16)
    l_term = jnp.einsum("bst,cst->bsc", columns, slope_cols, preferred_element_type=jnp.float32)
    l_term = (l_term * grad_scale).reshape(n_dp, -1, local_cols, BLOCKS)
    grad_l = ring_reduce_scatter(l_term, ring)
    grad_l = jnp.transpose(grad_l, (1, 0, 2)).reshape(local_cols, -1)
    back_rows = lax.all_to_all(back_cols, "feat", split_axis=1, concat_axis=0, tiled=True)
    through_r = jnp.einsum("obt,ibo->bit", back_rows, r_whole, preferred_element_type=jnp.float32)
    grad_x = (
        (g_blocks.astype(jnp.float32) + through_r)
        .astype(jnp.bfloat16)
        .reshape(local_blocks * WIDTH, tok_count)
    )
    r_term = (
        jnp.einsum("bit,obt->ibo", x_blocks, back_rows, preferred_element_type=jnp.float32)
        * grad_scale
    ).reshape(n_dp, rows_r, local_blocks, WIDTH)
    grad_r = ring_reduce_scatter(r_term, ring)
    grad_r = jnp.transpose(grad_r, (1, 0, 2))
    return (grad_x, grad_r, grad_l)


def solution(mesh):
    ring = ring_of(mesh)
    placed = (P("feat", "dp"), P("feat", "dp"), P("feat", "dp", None), P("feat", "dp"))
    return jax.shard_map(
        lambda *args: body(ring, *args),
        mesh=mesh,
        in_specs=placed,
        out_specs=(P("feat", "dp"), P("feat", "dp", None), P("feat", "dp")),
        check_vma=False,
    )
```

```python
import math

import jax
import jax.numpy as jnp
import numpy as np
from jax import lax
from jax.sharding import PartitionSpec as P

BLOCKS = 64
WIDTH = 256


def gelu_tanh(values):
    return jax.nn.gelu(values, approximate=True)


def slope_of(pre_act, upstream):
    _, pullback = jax.vjp(gelu_tanh, pre_act)
    return pullback(upstream.astype(jnp.float32))[0].astype(jnp.bfloat16)


def ring_of(mesh):
    row = mesh.devices[(slice(None),) + (0,) * (mesh.devices.ndim - 1)]
    size = len(row)
    try:
        spots = [tuple(d.coords) for d in row]
    except AttributeError:
        return list(range(size))
    near = [
        [j for j in range(size) if sum(abs(a - b) for a, b in zip(spots[i], spots[j])) == 1]
        for i in range(size)
    ]
    path, seen, budget = [0], {0}, [20000]

    def grow():
        budget[0] -= 1
        if budget[0] < 0:
            return False
        if len(path) == size:
            return 0 in near[path[-1]] or size <= 2
        here = path[-1]
        for nxt in sorted(near[here], key=lambda j: len([k for k in near[j] if k not in seen])):
            if nxt in seen:
                continue
            path.append(nxt)
            seen.add(nxt)
            if grow():
                return True
            path.pop()
            seen.discard(nxt)
        return False

    return list(path) if grow() else list(range(size))


def ring_reduce_scatter(parts, ring):
    n = len(ring)
    order = jnp.asarray(np.array(ring, np.int32))
    place = jnp.asarray(np.argsort(np.array(ring)).astype(np.int32))
    me = lax.axis_index("dp")
    here = place[me]
    forward = [(ring[p], ring[(p + 1) % n]) for p in range(n)]
    backward = [(ring[p], ring[(p - 1) % n]) for p in range(n)]
    total = lax.dynamic_index_in_dim(parts, me, axis=0, keepdims=False)
    ahead = n // 2
    for way, pairs, hops in ((1, forward, ahead), (-1, backward, n - 1 - ahead)):
        acc = None
        for step in range(hops):
            owner = order[(here + way * (hops - step)) % n]
            mine = lax.dynamic_index_in_dim(parts, owner, axis=0, keepdims=False)
            acc = lax.ppermute(mine if acc is None else acc + mine, "dp", pairs)
        total = total + acc
    return total

def ring_all_gather(piece, ring):
    n = len(ring)
    order = jnp.asarray(np.array(ring, np.int32))
    place = jnp.asarray(np.argsort(np.array(ring)).astype(np.int32))
    me = lax.axis_index("dp")
    here = place[me]
    forward = [(ring[p], ring[(p + 1) % n]) for p in range(n)]
    backward = [(ring[p], ring[(p - 1) % n]) for p in range(n)]
    held = lax.dynamic_update_index_in_dim(jnp.zeros((n,) + piece.shape, piece.dtype), piece, me, 0)
    ahead = n // 2
    for way, pairs, hops in ((1, forward, ahead), (-1, backward, n - 1 - ahead)):
        cur = piece
        for step in range(hops):
            cur = lax.ppermute(cur, "dp", pairs)
            owner = order[(here - way * (1 + step)) % n]
            held = lax.dynamic_update_index_in_dim(held, cur, owner, 0)
    return held

def body(ring, activations, cotangent, r_mix, l_mix):
    tok_count = activations.shape[1]
    local_blocks = activations.shape[0] // WIDTH
    n_dp = lax.axis_size("dp")
    grad_scale = 1.0 / math.sqrt(tok_count * n_dp)
    x_blocks = activations.reshape(local_blocks, WIDTH, tok_count)
    g_blocks = cotangent.reshape(local_blocks, WIDTH, tok_count)
    g_cols = lax.all_to_all(g_blocks, "feat", split_axis=1, concat_axis=0, tiled=True)
    local_cols = l_mix.shape[0]
    rows_r = r_mix.shape[1]
    r_lead = jnp.transpose(r_mix, (1, 0, 2)).reshape(-1, WIDTH)
    l_lead = jnp.transpose(l_mix.reshape(local_cols, -1, BLOCKS), (1, 0, 2)).reshape(-1, WIDTH)
    r_size = r_lead.shape[0]
    packed = jnp.concatenate([r_lead, l_lead], axis=0)
    packed = ring_all_gather(packed, ring)
    r_whole = packed[:, :r_size].reshape(n_dp * rows_r, local_blocks, WIDTH)
    l_blocks = packed[:, r_size:].reshape(-1, local_cols, BLOCKS)
    mixed_rows = jnp.einsum(
        "bit,ibo->bot", x_blocks, r_whole, preferred_element_type=jnp.float32
    ).astype(jnp.bfloat16)
    columns = lax.all_to_all(mixed_rows, "feat", split_axis=1, concat_axis=0, tiled=True)
    pre_act = jnp.einsum("bst,bsc->cst", columns, l_blocks, preferred_element_type=jnp.float32)
    slope_cols = slope_of(pre_act, g_cols)
    back_cols = jnp.einsum(
        "cst,bsc->sbt", slope_cols, l_blocks, preferred_element_type=jnp.float32
    ).astype(jnp.bfloat16)
    l_term = jnp.einsum("bst,cst->bsc", columns, slope_cols, preferred_element_type=jnp.float32)
    l_term = (l_term * grad_scale).reshape(n_dp, -1, local_cols, BLOCKS)
    grad_l = ring_reduce_scatter(l_term, ring)
    grad_l = jnp.transpose(grad_l, (1, 0, 2)).reshape(local_cols, -1)
    back_rows = lax.all_to_all(back_cols, "feat", split_axis=1, concat_axis=0, tiled=True)
    through_r = jnp.einsum("obt,ibo->bit", back_rows, r_whole, preferred_element_type=jnp.float32)
    grad_x = (
        (g_blocks.astype(jnp.float32) + through_r)
        .astype(jnp.bfloat16)
        .reshape(local_blocks * WIDTH, tok_count)
    )
    r_term = (
        jnp.einsum("bit,obt->ibo", x_blocks, back_rows, preferred_element_type=jnp.float32)
        * grad_scale
    ).reshape(n_dp, rows_r, local_blocks, WIDTH)
    grad_r = ring_reduce_scatter(r_term, ring)
    grad_r = jnp.transpose(grad_r, (1, 0, 2))
    return (grad_x, grad_r, grad_l)


def solution(mesh):
    ring = ring_of(mesh)
    placed = (P("feat", "dp"), P("feat", "dp"), P("feat", "dp", None), P("feat", "dp"))
    return jax.shard_map(
        lambda *args: body(ring, *args),
        mesh=mesh,
        in_specs=placed,
        out_specs=(P("feat", "dp"), P("feat", "dp", None), P("feat", "dp")),
        check_vma=False,
    )
```

```python
import math

import jax
import jax.numpy as jnp
import numpy as np
from jax import lax
from jax.sharding import PartitionSpec as P

BLOCKS = 64
WIDTH = 256


def gelu_tanh(values):
    return jax.nn.gelu(values, approximate=True)


def slope_of(pre_act, upstream):
    _, pullback = jax.vjp(gelu_tanh, pre_act)
    return pullback(upstream.astype(jnp.float32))[0].astype(jnp.bfloat16)


def ring_of(mesh):
    row = mesh.devices[(slice(None),) + (0,) * (mesh.devices.ndim - 1)]
    size = len(row)
    try:
        spots = [tuple(d.coords) for d in row]
    except AttributeError:
        return list(range(size))
    near = [
        [j for j in range(size) if sum(abs(a - b) for a, b in zip(spots[i], spots[j])) == 1]
        for i in range(size)
    ]
    path, seen, budget = [0], {0}, [20000]

    def grow():
        budget[0] -= 1
        if budget[0] < 0:
            return False
        if len(path) == size:
            return 0 in near[path[-1]] or size <= 2
        here = path[-1]
        for nxt in sorted(near[here], key=lambda j: len([k for k in near[j] if k not in seen])):
            if nxt in seen:
                continue
            path.append(nxt)
            seen.add(nxt)
            if grow():
                return True
            path.pop()
            seen.discard(nxt)
        return False

    return list(path) if grow() else list(range(size))


def ring_reduce_scatter(parts, ring):
    n = len(ring)
    order = jnp.asarray(np.array(ring, np.int32))
    place = jnp.asarray(np.argsort(np.array(ring)).astype(np.int32))
    me = lax.axis_index("dp")
    here = place[me]
    forward = [(ring[p], ring[(p + 1) % n]) for p in range(n)]
    backward = [(ring[p], ring[(p - 1) % n]) for p in range(n)]
    half = parts.shape[1] // 2
    sides = (parts[:, :half], parts[:, half:])
    totals = [lax.dynamic_index_in_dim(side, me, axis=0, keepdims=False) for side in sides]
    ahead, behind = n // 2, n - 1 - n // 2
    for way, pairs, hops in ((1, forward, (ahead, behind)), (-1, backward, (behind, ahead))):
        accs = [None, None]
        for step in range(max(hops)):
            live = [k for k in range(2) if step < hops[k]]
            for k in live:
                owner = order[(here + way * (hops[k] - step)) % n]
                mine = lax.dynamic_index_in_dim(sides[k], owner, axis=0, keepdims=False)
                accs[k] = mine if accs[k] is None else accs[k] + mine
            sent = lax.ppermute(jnp.stack([accs[k] for k in live]), "dp", pairs)
            for i, k in enumerate(live):
                accs[k] = sent[i]
        totals = [t + a for t, a in zip(totals, accs)]
    return jnp.concatenate(totals, axis=0)

def ring_all_gather(piece, ring):
    n = len(ring)
    order = jnp.asarray(np.array(ring, np.int32))
    place = jnp.asarray(np.argsort(np.array(ring)).astype(np.int32))
    me = lax.axis_index("dp")
    here = place[me]
    forward = [(ring[p], ring[(p + 1) % n]) for p in range(n)]
    backward = [(ring[p], ring[(p - 1) % n]) for p in range(n)]
    held = lax.dynamic_update_index_in_dim(jnp.zeros((n,) + piece.shape, piece.dtype), piece, me, 0)
    ahead = n // 2
    for way, pairs, hops in ((1, forward, ahead), (-1, backward, n - 1 - ahead)):
        cur = piece
        for step in range(hops):
            cur = lax.ppermute(cur, "dp", pairs)
            owner = order[(here - way * (1 + step)) % n]
            held = lax.dynamic_update_index_in_dim(held, cur, owner, 0)
    return held

def body(ring, activations, cotangent, r_mix, l_mix):
    tok_count = activations.shape[1]
    local_blocks = activations.shape[0] // WIDTH
    n_dp = lax.axis_size("dp")
    grad_scale = 1.0 / math.sqrt(tok_count * n_dp)
    x_blocks = activations.reshape(local_blocks, WIDTH, tok_count)
    g_blocks = cotangent.reshape(local_blocks, WIDTH, tok_count)
    g_cols = lax.all_to_all(g_blocks, "feat", split_axis=1, concat_axis=0, tiled=True)
    local_cols = l_mix.shape[0]
    rows_r = r_mix.shape[1]
    r_lead = jnp.transpose(r_mix, (1, 0, 2)).reshape(-1, WIDTH)
    l_lead = jnp.transpose(l_mix.reshape(local_cols, -1, BLOCKS), (1, 0, 2)).reshape(-1, WIDTH)
    r_size = r_lead.shape[0]
    packed = jnp.concatenate([r_lead, l_lead], axis=0)
    packed = ring_all_gather(packed, ring)
    r_whole = packed[:, :r_size].reshape(n_dp * rows_r, local_blocks, WIDTH)
    l_blocks = packed[:, r_size:].reshape(-1, local_cols, BLOCKS)
    mixed_rows = jnp.einsum(
        "bit,ibo->bot", x_blocks, r_whole, preferred_element_type=jnp.float32
    ).astype(jnp.bfloat16)
    columns = lax.all_to_all(mixed_rows, "feat", split_axis=1, concat_axis=0, tiled=True)
    pre_act = jnp.einsum("bst,bsc->cst", columns, l_blocks, preferred_element_type=jnp.float32)
    slope_cols = slope_of(pre_act, g_cols)
    back_cols = jnp.einsum(
        "cst,bsc->sbt", slope_cols, l_blocks, preferred_element_type=jnp.float32
    ).astype(jnp.bfloat16)
    l_term = jnp.einsum("bst,cst->bsc", columns, slope_cols, preferred_element_type=jnp.float32)
    l_term = (l_term * grad_scale).reshape(n_dp, -1, local_cols, BLOCKS)
    grad_l = ring_reduce_scatter(l_term, ring)
    grad_l = jnp.transpose(grad_l, (1, 0, 2)).reshape(local_cols, -1)
    back_rows = lax.all_to_all(back_cols, "feat", split_axis=1, concat_axis=0, tiled=True)
    through_r = jnp.einsum("obt,ibo->bit", back_rows, r_whole, preferred_element_type=jnp.float32)
    grad_x = (
        (g_blocks.astype(jnp.float32) + through_r)
        .astype(jnp.bfloat16)
        .reshape(local_blocks * WIDTH, tok_count)
    )
    r_term = (
        jnp.einsum("bit,obt->ibo", x_blocks, back_rows, preferred_element_type=jnp.float32)
        * grad_scale
    ).reshape(n_dp, rows_r, local_blocks, WIDTH)
    grad_r = ring_reduce_scatter(r_term, ring)
    grad_r = jnp.transpose(grad_r, (1, 0, 2))
    return (grad_x, grad_r, grad_l)


def solution(mesh):
    ring = ring_of(mesh)
    placed = (P("feat", "dp"), P("feat", "dp"), P("feat", "dp", None), P("feat", "dp"))
    return jax.shard_map(
        lambda *args: body(ring, *args),
        mesh=mesh,
        in_specs=placed,
        out_specs=(P("feat", "dp"), P("feat", "dp", None), P("feat", "dp")),
        check_vma=False,
    )
```

```python
import math

import jax
import jax.numpy as jnp
import numpy as np
from jax import lax
from jax.sharding import PartitionSpec as P

BLOCKS = 64
WIDTH = 256


def gelu_tanh(values):
    return jax.nn.gelu(values, approximate=True)


def slope_of(pre_act, upstream):
    _, pullback = jax.vjp(gelu_tanh, pre_act)
    return pullback(upstream.astype(jnp.float32))[0].astype(jnp.bfloat16)


def ring_of(mesh):
    row = mesh.devices[(slice(None),) + (0,) * (mesh.devices.ndim - 1)]
    size = len(row)
    try:
        spots = [tuple(d.coords) for d in row]
    except AttributeError:
        return list(range(size))
    near = [
        [j for j in range(size) if sum(abs(a - b) for a, b in zip(spots[i], spots[j])) == 1]
        for i in range(size)
    ]
    path, seen, budget = [0], {0}, [20000]

    def grow():
        budget[0] -= 1
        if budget[0] < 0:
            return False
        if len(path) == size:
            return 0 in near[path[-1]] or size <= 2
        here = path[-1]
        for nxt in sorted(near[here], key=lambda j: len([k for k in near[j] if k not in seen])):
            if nxt in seen:
                continue
            path.append(nxt)
            seen.add(nxt)
            if grow():
                return True
            path.pop()
            seen.discard(nxt)
        return False

    return list(path) if grow() else list(range(size))


def ring_reduce_scatter(parts, ring):
    n = len(ring)
    order = jnp.asarray(np.array(ring, np.int32))
    place = jnp.asarray(np.argsort(np.array(ring)).astype(np.int32))
    me = lax.axis_index("dp")
    here = place[me]
    forward = [(ring[p], ring[(p + 1) % n]) for p in range(n)]
    backward = [(ring[p], ring[(p - 1) % n]) for p in range(n)]
    total = lax.dynamic_index_in_dim(parts, me, axis=0, keepdims=False)
    ahead = n // 2
    for way, pairs, hops in ((1, forward, ahead), (-1, backward, n - 1 - ahead)):
        acc = None
        for step in range(hops):
            owner = order[(here + way * (hops - step)) % n]
            mine = lax.dynamic_index_in_dim(parts, owner, axis=0, keepdims=False)
            acc = lax.ppermute(mine if acc is None else acc + mine, "dp", pairs)
        total = total + acc
    return total

def ring_all_gather(piece, ring):
    n = len(ring)
    order = jnp.asarray(np.array(ring, np.int32))
    place = jnp.asarray(np.argsort(np.array(ring)).astype(np.int32))
    me = lax.axis_index("dp")
    here = place[me]
    forward = [(ring[p], ring[(p + 1) % n]) for p in range(n)]
    backward = [(ring[p], ring[(p - 1) % n]) for p in range(n)]
    held = lax.dynamic_update_index_in_dim(jnp.zeros((n,) + piece.shape, piece.dtype), piece, me, 0)
    ahead = n // 2
    for way, pairs, hops in ((1, forward, ahead), (-1, backward, n - 1 - ahead)):
        cur = piece
        for step in range(hops):
            cur = lax.ppermute(cur, "dp", pairs)
            owner = order[(here - way * (1 + step)) % n]
            held = lax.dynamic_update_index_in_dim(held, cur, owner, 0)
    return held

def permute_all_to_all(blocks, axis):
    n = lax.axis_size("feat")
    me = lax.axis_index("feat")
    pieces = jnp.stack(jnp.split(blocks, n, axis=axis))
    by_shift = [lax.dynamic_index_in_dim(pieces, me, axis=0, keepdims=False)]
    for shift in range(1, n):
        mine = lax.dynamic_index_in_dim(pieces, (me + shift) % n, axis=0, keepdims=False)
        by_shift.append(lax.ppermute(mine, "feat", [(f, (f + shift) % n) for f in range(n)]))
    by_shift = jnp.stack(by_shift)
    came = [lax.dynamic_index_in_dim(by_shift, (me - src) % n, axis=0, keepdims=False) for src in range(n)]
    return jnp.concatenate(came, axis=0)


def body(ring, activations, cotangent, r_mix, l_mix):
    tok_count = activations.shape[1]
    local_blocks = activations.shape[0] // WIDTH
    n_dp = lax.axis_size("dp")
    grad_scale = 1.0 / math.sqrt(tok_count * n_dp)
    x_blocks = activations.reshape(local_blocks, WIDTH, tok_count)
    g_blocks = cotangent.reshape(local_blocks, WIDTH, tok_count)
    g_cols = permute_all_to_all(g_blocks, 1)
    local_cols = l_mix.shape[0]
    rows_r = r_mix.shape[1]
    r_lead = jnp.transpose(r_mix, (1, 0, 2)).reshape(-1, WIDTH)
    l_lead = jnp.transpose(l_mix.reshape(local_cols, -1, BLOCKS), (1, 0, 2)).reshape(-1, WIDTH)
    r_size = r_lead.shape[0]
    packed = jnp.concatenate([r_lead, l_lead], axis=0)
    packed = ring_all_gather(packed, ring)
    r_whole = packed[:, :r_size].reshape(n_dp * rows_r, local_blocks, WIDTH)
    l_blocks = packed[:, r_size:].reshape(-1, local_cols, BLOCKS)
    mixed_rows = jnp.einsum(
        "bit,ibo->bot", x_blocks, r_whole, preferred_element_type=jnp.float32
    ).astype(jnp.bfloat16)
    columns = lax.all_to_all(mixed_rows, "feat", split_axis=1, concat_axis=0, tiled=True)
    pre_act = jnp.einsum("bst,bsc->cst", columns, l_blocks, preferred_element_type=jnp.float32)
    slope_cols = slope_of(pre_act, g_cols)
    back_cols = jnp.einsum(
        "cst,bsc->sbt", slope_cols, l_blocks, preferred_element_type=jnp.float32
    ).astype(jnp.bfloat16)
    l_term = jnp.einsum("bst,cst->bsc", columns, slope_cols, preferred_element_type=jnp.float32)
    l_term = (l_term * grad_scale).reshape(n_dp, -1, local_cols, BLOCKS)
    grad_l = ring_reduce_scatter(l_term, ring)
    grad_l = jnp.transpose(grad_l, (1, 0, 2)).reshape(local_cols, -1)
    back_rows = lax.all_to_all(back_cols, "feat", split_axis=1, concat_axis=0, tiled=True)
    through_r = jnp.einsum("obt,ibo->bit", back_rows, r_whole, preferred_element_type=jnp.float32)
    grad_x = (
        (g_blocks.astype(jnp.float32) + through_r)
        .astype(jnp.bfloat16)
        .reshape(local_blocks * WIDTH, tok_count)
    )
    r_term = (
        jnp.einsum("bit,obt->ibo", x_blocks, back_rows, preferred_element_type=jnp.float32)
        * grad_scale
    ).reshape(n_dp, rows_r, local_blocks, WIDTH)
    grad_r = ring_reduce_scatter(r_term, ring)
    grad_r = jnp.transpose(grad_r, (1, 0, 2))
    return (grad_x, grad_r, grad_l)


def solution(mesh):
    ring = ring_of(mesh)
    placed = (P("feat", "dp"), P("feat", "dp"), P("feat", "dp", None), P("feat", "dp"))
    return jax.shard_map(
        lambda *args: body(ring, *args),
        mesh=mesh,
        in_specs=placed,
        out_specs=(P("feat", "dp"), P("feat", "dp", None), P("feat", "dp")),
        check_vma=False,
    )
```

```python
import math

import jax
import jax.numpy as jnp
import numpy as np
from jax import lax
from jax.sharding import PartitionSpec as P

BLOCKS = 64
WIDTH = 256


def gelu_tanh(values):
    return jax.nn.gelu(values, approximate=True)


def slope_of(pre_act, upstream):
    _, pullback = jax.vjp(gelu_tanh, pre_act)
    return pullback(upstream.astype(jnp.float32))[0].astype(jnp.bfloat16)


def ring_of(mesh):
    row = mesh.devices[(slice(None),) + (0,) * (mesh.devices.ndim - 1)]
    size = len(row)
    try:
        spots = [tuple(d.coords) for d in row]
    except AttributeError:
        return list(range(size))
    near = [
        [j for j in range(size) if sum(abs(a - b) for a, b in zip(spots[i], spots[j])) == 1]
        for i in range(size)
    ]
    path, seen, budget = [0], {0}, [20000]

    def grow():
        budget[0] -= 1
        if budget[0] < 0:
            return False
        if len(path) == size:
            return 0 in near[path[-1]] or size <= 2
        here = path[-1]
        for nxt in sorted(near[here], key=lambda j: len([k for k in near[j] if k not in seen])):
            if nxt in seen:
                continue
            path.append(nxt)
            seen.add(nxt)
            if grow():
                return True
            path.pop()
            seen.discard(nxt)
        return False

    return list(path) if grow() else list(range(size))


def ring_reduce_scatter(parts, ring):
    n = len(ring)
    order = jnp.asarray(np.array(ring, np.int32))
    place = jnp.asarray(np.argsort(np.array(ring)).astype(np.int32))
    me = lax.axis_index("dp")
    here = place[me]
    forward = [(ring[p], ring[(p + 1) % n]) for p in range(n)]
    backward = [(ring[p], ring[(p - 1) % n]) for p in range(n)]
    total = lax.dynamic_index_in_dim(parts, me, axis=0, keepdims=False)
    ahead = n // 2
    for way, pairs, hops in ((1, forward, ahead), (-1, backward, n - 1 - ahead)):
        acc = None
        for step in range(hops):
            owner = order[(here + way * (hops - step)) % n]
            mine = lax.dynamic_index_in_dim(parts, owner, axis=0, keepdims=False)
            acc = lax.ppermute(mine if acc is None else acc + mine, "dp", pairs)
        total = total + acc
    return total

def ring_all_gather(piece, ring):
    n = len(ring)
    order = jnp.asarray(np.array(ring, np.int32))
    place = jnp.asarray(np.argsort(np.array(ring)).astype(np.int32))
    me = lax.axis_index("dp")
    here = place[me]
    forward = [(ring[p], ring[(p + 1) % n]) for p in range(n)]
    backward = [(ring[p], ring[(p - 1) % n]) for p in range(n)]
    held = lax.dynamic_update_index_in_dim(jnp.zeros((n,) + piece.shape, piece.dtype), piece, me, 0)
    ahead = n // 2
    for way, pairs, hops in ((1, forward, ahead), (-1, backward, n - 1 - ahead)):
        cur = piece
        for step in range(hops):
            cur = lax.ppermute(cur, "dp", pairs)
            owner = order[(here - way * (1 + step)) % n]
            held = lax.dynamic_update_index_in_dim(held, cur, owner, 0)
    return held

def body(ring, activations, cotangent, r_mix, l_mix):
    tok_count = activations.shape[1]
    local_blocks = activations.shape[0] // WIDTH
    n_dp = lax.axis_size("dp")
    grad_scale = 1.0 / math.sqrt(tok_count * n_dp)
    x_blocks = activations.reshape(local_blocks, WIDTH, tok_count)
    g_blocks = cotangent.reshape(local_blocks, WIDTH, tok_count)
    g_cols = lax.all_to_all(g_blocks, "feat", split_axis=1, concat_axis=0, tiled=True)
    local_cols = l_mix.shape[0]
    rows_r = r_mix.shape[1]
    r_lead = jnp.transpose(r_mix, (1, 0, 2)).reshape(-1, WIDTH)
    l_lead = jnp.transpose(l_mix.reshape(local_cols, -1, BLOCKS), (1, 0, 2)).reshape(-1, WIDTH)
    r_size = r_lead.shape[0]
    packed = jnp.concatenate([r_lead, l_lead], axis=0)
    packed = ring_all_gather(packed, ring)
    r_whole = packed[:, :r_size].reshape(n_dp * rows_r, local_blocks, WIDTH)
    l_blocks = packed[:, r_size:].reshape(-1, local_cols, BLOCKS)
    mixed_rows = jnp.einsum(
        "bit,ibo->bot", x_blocks, r_whole, preferred_element_type=jnp.float32
    ).astype(jnp.bfloat16)
    columns = lax.all_to_all(mixed_rows, "feat", split_axis=1, concat_axis=0, tiled=True)
    pre_act = jnp.einsum("bst,bsc->cst", columns, l_blocks, preferred_element_type=jnp.float32)
    slope_cols = slope_of(pre_act, g_cols)
    back_cols = jnp.einsum(
        "cst,bsc->sbt", slope_cols, l_blocks, preferred_element_type=jnp.float32
    ).astype(jnp.bfloat16)
    l_term = jnp.einsum("bst,cst->bsc", columns, slope_cols, preferred_element_type=jnp.float32)
    l_term = (l_term * grad_scale).reshape(n_dp, -1, WIDTH)
    back_rows = lax.all_to_all(back_cols, "feat", split_axis=1, concat_axis=0, tiled=True)
    through_r = jnp.einsum("obt,ibo->bit", back_rows, r_whole, preferred_element_type=jnp.float32)
    grad_x = (
        (g_blocks.astype(jnp.float32) + through_r)
        .astype(jnp.bfloat16)
        .reshape(local_blocks * WIDTH, tok_count)
    )
    r_term = (
        jnp.einsum("bit,obt->ibo", x_blocks, back_rows, preferred_element_type=jnp.float32)
        * grad_scale
    ).reshape(n_dp, rows_r * local_blocks, WIDTH)
    summed = ring_reduce_scatter(jnp.concatenate([r_term, l_term], axis=1), ring)
    r_rows = r_term.shape[1]
    grad_r = jnp.transpose(summed[:r_rows].reshape(rows_r, local_blocks, WIDTH), (1, 0, 2))
    grad_l = summed[r_rows:].reshape(-1, local_cols, BLOCKS)
    grad_l = jnp.transpose(grad_l, (1, 0, 2)).reshape(local_cols, -1)
    return (grad_x, grad_r, grad_l)


def solution(mesh):
    ring = ring_of(mesh)
    placed = (P("feat", "dp"), P("feat", "dp"), P("feat", "dp", None), P("feat", "dp"))
    return jax.shard_map(
        lambda *args: body(ring, *args),
        mesh=mesh,
        in_specs=placed,
        out_specs=(P("feat", "dp"), P("feat", "dp", None), P("feat", "dp")),
        check_vma=False,
    )
```

```python
import math

import jax
import jax.numpy as jnp
import numpy as np
from jax import lax
from jax.sharding import PartitionSpec as P

BLOCKS = 64
WIDTH = 256


def gelu_tanh(values):
    return jax.nn.gelu(values, approximate=True)


def slope_of(pre_act, upstream):
    _, pullback = jax.vjp(gelu_tanh, pre_act)
    return pullback(upstream.astype(jnp.float32))[0].astype(jnp.bfloat16)


def ring_of(mesh):
    row = mesh.devices[(slice(None),) + (0,) * (mesh.devices.ndim - 1)]
    size = len(row)
    try:
        spots = [tuple(d.coords) for d in row]
    except AttributeError:
        return list(range(size))
    near = [
        [j for j in range(size) if sum(abs(a - b) for a, b in zip(spots[i], spots[j])) == 1]
        for i in range(size)
    ]
    path, seen, budget = [0], {0}, [20000]

    def grow():
        budget[0] -= 1
        if budget[0] < 0:
            return False
        if len(path) == size:
            return 0 in near[path[-1]] or size <= 2
        here = path[-1]
        for nxt in sorted(near[here], key=lambda j: len([k for k in near[j] if k not in seen])):
            if nxt in seen:
                continue
            path.append(nxt)
            seen.add(nxt)
            if grow():
                return True
            path.pop()
            seen.discard(nxt)
        return False

    return list(path) if grow() else list(range(size))


def ring_reduce_scatter(parts, ring):
    n = len(ring)
    order = jnp.asarray(np.array(ring, np.int32))
    place = jnp.asarray(np.argsort(np.array(ring)).astype(np.int32))
    me = lax.axis_index("dp")
    here = place[me]
    forward = [(ring[p], ring[(p + 1) % n]) for p in range(n)]
    backward = [(ring[p], ring[(p - 1) % n]) for p in range(n)]
    total = lax.dynamic_index_in_dim(parts, me, axis=0, keepdims=False)
    ahead = n // 2
    for way, pairs, hops in ((1, forward, ahead), (-1, backward, n - 1 - ahead)):
        acc = None
        for step in range(hops):
            owner = order[(here + way * (hops - step)) % n]
            mine = lax.dynamic_index_in_dim(parts, owner, axis=0, keepdims=False)
            acc = lax.ppermute(mine if acc is None else acc + mine, "dp", pairs)
        total = total + acc
    return total

def ring_all_gather(piece, ring):
    n = len(ring)
    order = jnp.asarray(np.array(ring, np.int32))
    place = jnp.asarray(np.argsort(np.array(ring)).astype(np.int32))
    me = lax.axis_index("dp")
    here = place[me]
    forward = [(ring[p], ring[(p + 1) % n]) for p in range(n)]
    backward = [(ring[p], ring[(p - 1) % n]) for p in range(n)]
    held = lax.dynamic_update_index_in_dim(jnp.zeros((n,) + piece.shape, piece.dtype), piece, me, 0)
    ahead = n // 2
    for way, pairs, hops in ((1, forward, ahead), (-1, backward, n - 1 - ahead)):
        cur = piece
        for step in range(hops):
            cur = lax.ppermute(cur, "dp", pairs)
            owner = order[(here - way * (1 + step)) % n]
            held = lax.dynamic_update_index_in_dim(held, cur, owner, 0)
    return held

def body(ring, activations, cotangent, r_mix, l_mix):
    tok_count = activations.shape[1]
    local_blocks = activations.shape[0] // WIDTH
    n_dp = lax.axis_size("dp")
    grad_scale = 1.0 / math.sqrt(tok_count * n_dp)
    x_blocks = activations.reshape(local_blocks, WIDTH, tok_count)
    g_blocks = cotangent.reshape(local_blocks, WIDTH, tok_count)
    g_cols = lax.all_to_all(g_blocks, "feat", split_axis=1, concat_axis=0, tiled=True)
    local_cols = l_mix.shape[0]
    rows_r = r_mix.shape[1]
    r_lead = jnp.transpose(r_mix, (1, 0, 2)).reshape(-1, WIDTH)
    l_lead = jnp.transpose(l_mix.reshape(local_cols, -1, BLOCKS), (1, 0, 2)).reshape(-1, WIDTH)
    r_size = r_lead.shape[0]
    packed = jnp.concatenate([r_lead, l_lead], axis=0)
    packed = ring_all_gather(packed, ring)
    r_whole = packed[:, :r_size].reshape(n_dp * rows_r, local_blocks, WIDTH)
    l_blocks = packed[:, r_size:].reshape(-1, local_cols, BLOCKS)
    cut = tok_count // 2
    l_term = r_term = None
    xs = []
    for lo, hi in ((0, cut), (cut, tok_count)):
        x_half = x_blocks[:, :, lo:hi]
        mixed_rows = jnp.einsum(
            "bit,ibo->bot", x_half, r_whole, preferred_element_type=jnp.float32
        ).astype(jnp.bfloat16)
        columns = lax.all_to_all(mixed_rows, "feat", split_axis=1, concat_axis=0, tiled=True)
        pre_act = jnp.einsum("bst,bsc->cst", columns, l_blocks, preferred_element_type=jnp.float32)
        slope_cols = slope_of(pre_act, g_cols[:, :, lo:hi])
        back_cols = jnp.einsum(
            "cst,bsc->sbt", slope_cols, l_blocks, preferred_element_type=jnp.float32
        ).astype(jnp.bfloat16)
        l_part = jnp.einsum("bst,cst->bsc", columns, slope_cols, preferred_element_type=jnp.float32)
        l_term = l_part if l_term is None else l_term + l_part
        back_rows = lax.all_to_all(back_cols, "feat", split_axis=1, concat_axis=0, tiled=True)
        through_r = jnp.einsum("obt,ibo->bit", back_rows, r_whole, preferred_element_type=jnp.float32)
        xs.append((g_blocks[:, :, lo:hi].astype(jnp.float32) + through_r).astype(jnp.bfloat16))
        r_part = jnp.einsum("bit,obt->ibo", x_half, back_rows, preferred_element_type=jnp.float32)
        r_term = r_part if r_term is None else r_term + r_part
    grad_x = jnp.concatenate(xs, axis=2).reshape(local_blocks * WIDTH, tok_count)
    l_term = (l_term * grad_scale).reshape(n_dp, -1, local_cols, BLOCKS)
    grad_l = ring_reduce_scatter(l_term, ring)
    grad_l = jnp.transpose(grad_l, (1, 0, 2)).reshape(local_cols, -1)
    r_term = (r_term * grad_scale).reshape(n_dp, rows_r, local_blocks, WIDTH)
    grad_r = ring_reduce_scatter(r_term, ring)
    grad_r = jnp.transpose(grad_r, (1, 0, 2))
    return (grad_x, grad_r, grad_l)


def solution(mesh):
    ring = ring_of(mesh)
    placed = (P("feat", "dp"), P("feat", "dp"), P("feat", "dp", None), P("feat", "dp"))
    return jax.shard_map(
        lambda *args: body(ring, *args),
        mesh=mesh,
        in_specs=placed,
        out_specs=(P("feat", "dp"), P("feat", "dp", None), P("feat", "dp")),
        check_vma=False,
    )
```

```python
import math

import jax
import jax.numpy as jnp
import numpy as np
from jax import lax
from jax.sharding import PartitionSpec as P

BLOCKS = 64
WIDTH = 256


def gelu_tanh(values):
    return jax.nn.gelu(values, approximate=True)


def slope_of(pre_act, upstream):
    _, pullback = jax.vjp(gelu_tanh, pre_act)
    return pullback(upstream.astype(jnp.float32))[0].astype(jnp.bfloat16)


def ring_of(mesh):
    row = mesh.devices[(slice(None),) + (0,) * (mesh.devices.ndim - 1)]
    size = len(row)
    try:
        spots = [tuple(d.coords) for d in row]
    except AttributeError:
        return list(range(size))
    near = [
        [j for j in range(size) if sum(abs(a - b) for a, b in zip(spots[i], spots[j])) == 1]
        for i in range(size)
    ]
    path, seen, budget = [0], {0}, [20000]

    def grow():
        budget[0] -= 1
        if budget[0] < 0:
            return False
        if len(path) == size:
            return 0 in near[path[-1]] or size <= 2
        here = path[-1]
        for nxt in sorted(near[here], key=lambda j: len([k for k in near[j] if k not in seen])):
            if nxt in seen:
                continue
            path.append(nxt)
            seen.add(nxt)
            if grow():
                return True
            path.pop()
            seen.discard(nxt)
        return False

    return list(path) if grow() else list(range(size))


def ring_reduce_scatter(parts, ring, lead=1):
    n = len(ring)
    order = jnp.asarray(np.array(ring, np.int32))
    place = jnp.asarray(np.argsort(np.array(ring)).astype(np.int32))
    me = lax.axis_index("dp")
    here = place[me]
    forward = [(ring[p], ring[(p + 1) % n]) for p in range(n)]
    backward = [(ring[p], ring[(p - 1) % n]) for p in range(n)]
    total = lax.dynamic_index_in_dim(parts, me, axis=0, keepdims=False)
    ahead = n // 2 if lead > 0 else n - 1 - n // 2
    for way, pairs, hops in ((1, forward, ahead), (-1, backward, n - 1 - ahead)):
        acc = None
        for step in range(hops):
            owner = order[(here + way * (hops - step)) % n]
            mine = lax.dynamic_index_in_dim(parts, owner, axis=0, keepdims=False)
            acc = lax.ppermute(mine if acc is None else acc + mine, "dp", pairs)
        total = total + acc
    return total

def ring_all_gather(piece, ring):
    n = len(ring)
    order = jnp.asarray(np.array(ring, np.int32))
    place = jnp.asarray(np.argsort(np.array(ring)).astype(np.int32))
    me = lax.axis_index("dp")
    here = place[me]
    forward = [(ring[p], ring[(p + 1) % n]) for p in range(n)]
    backward = [(ring[p], ring[(p - 1) % n]) for p in range(n)]
    held = lax.dynamic_update_index_in_dim(jnp.zeros((n,) + piece.shape, piece.dtype), piece, me, 0)
    ahead = n // 2
    for way, pairs, hops in ((1, forward, ahead), (-1, backward, n - 1 - ahead)):
        cur = piece
        for step in range(hops):
            cur = lax.ppermute(cur, "dp", pairs)
            owner = order[(here - way * (1 + step)) % n]
            held = lax.dynamic_update_index_in_dim(held, cur, owner, 0)
    return held

def body(ring, activations, cotangent, r_mix, l_mix):
    tok_count = activations.shape[1]
    local_blocks = activations.shape[0] // WIDTH
    n_dp = lax.axis_size("dp")
    grad_scale = 1.0 / math.sqrt(tok_count * n_dp)
    x_blocks = activations.reshape(local_blocks, WIDTH, tok_count)
    g_blocks = cotangent.reshape(local_blocks, WIDTH, tok_count)
    g_cols = lax.all_to_all(g_blocks, "feat", split_axis=1, concat_axis=0, tiled=True)
    local_cols = l_mix.shape[0]
    rows_r = r_mix.shape[1]
    r_lead = jnp.transpose(r_mix, (1, 0, 2)).reshape(-1, WIDTH)
    l_lead = jnp.transpose(l_mix.reshape(local_cols, -1, BLOCKS), (1, 0, 2)).reshape(-1, WIDTH)
    r_size = r_lead.shape[0]
    packed = jnp.concatenate([r_lead, l_lead], axis=0)
    packed = ring_all_gather(packed, ring)
    r_whole = packed[:, :r_size].reshape(n_dp * rows_r, local_blocks, WIDTH)
    l_blocks = packed[:, r_size:].reshape(-1, local_cols, BLOCKS)
    mixed_rows = jnp.einsum(
        "bit,ibo->bot", x_blocks, r_whole, preferred_element_type=jnp.float32
    ).astype(jnp.bfloat16)
    columns = lax.all_to_all(mixed_rows, "feat", split_axis=1, concat_axis=0, tiled=True)
    pre_act = jnp.einsum("bst,bsc->cst", columns, l_blocks, preferred_element_type=jnp.float32)
    slope_cols = slope_of(pre_act, g_cols)
    back_cols = jnp.einsum(
        "cst,bsc->sbt", slope_cols, l_blocks, preferred_element_type=jnp.float32
    ).astype(jnp.bfloat16)
    l_term = jnp.einsum("bst,cst->bsc", columns, slope_cols, preferred_element_type=jnp.float32)
    l_term = (l_term * grad_scale).reshape(n_dp, -1, local_cols, BLOCKS)
    grad_l = ring_reduce_scatter(l_term, ring, lead=-1)
    grad_l = jnp.transpose(grad_l, (1, 0, 2)).reshape(local_cols, -1)
    back_rows = lax.all_to_all(back_cols, "feat", split_axis=1, concat_axis=0, tiled=True)
    through_r = jnp.einsum("obt,ibo->bit", back_rows, r_whole, preferred_element_type=jnp.float32)
    grad_x = (
        (g_blocks.astype(jnp.float32) + through_r)
        .astype(jnp.bfloat16)
        .reshape(local_blocks * WIDTH, tok_count)
    )
    r_term = (
        jnp.einsum("bit,obt->ibo", x_blocks, back_rows, preferred_element_type=jnp.float32)
        * grad_scale
    ).reshape(n_dp, rows_r, local_blocks, WIDTH)
    grad_r = ring_reduce_scatter(r_term, ring)
    grad_r = jnp.transpose(grad_r, (1, 0, 2))
    return (grad_x, grad_r, grad_l)


def solution(mesh):
    ring = ring_of(mesh)
    placed = (P("feat", "dp"), P("feat", "dp"), P("feat", "dp", None), P("feat", "dp"))
    return jax.shard_map(
        lambda *args: body(ring, *args),
        mesh=mesh,
        in_specs=placed,
        out_specs=(P("feat", "dp"), P("feat", "dp", None), P("feat", "dp")),
        check_vma=False,
    )
```

```python
import math

import jax
import jax.numpy as jnp
import numpy as np
from jax import lax
from jax.sharding import PartitionSpec as P

BLOCKS = 64
WIDTH = 256


def gelu_tanh(values):
    return jax.nn.gelu(values, approximate=True)


def slope_of(pre_act, upstream):
    _, pullback = jax.vjp(gelu_tanh, pre_act)
    return pullback(upstream.astype(jnp.float32))[0].astype(jnp.bfloat16)


def ring_of(mesh):
    row = mesh.devices[(slice(None),) + (0,) * (mesh.devices.ndim - 1)]
    size = len(row)
    try:
        spots = [tuple(d.coords) for d in row]
    except AttributeError:
        return list(range(size))
    near = [
        [j for j in range(size) if sum(abs(a - b) for a, b in zip(spots[i], spots[j])) == 1]
        for i in range(size)
    ]
    path, seen, budget = [0], {0}, [20000]

    def grow():
        budget[0] -= 1
        if budget[0] < 0:
            return False
        if len(path) == size:
            return 0 in near[path[-1]] or size <= 2
        here = path[-1]
        for nxt in sorted(near[here], key=lambda j: len([k for k in near[j] if k not in seen])):
            if nxt in seen:
                continue
            path.append(nxt)
            seen.add(nxt)
            if grow():
                return True
            path.pop()
            seen.discard(nxt)
        return False

    return list(path) if grow() else list(range(size))


def ring_reduce_scatter(parts, ring, lead=1):
    n = len(ring)
    order = jnp.asarray(np.array(ring, np.int32))
    place = jnp.asarray(np.argsort(np.array(ring)).astype(np.int32))
    me = lax.axis_index("dp")
    here = place[me]
    forward = [(ring[p], ring[(p + 1) % n]) for p in range(n)]
    backward = [(ring[p], ring[(p - 1) % n]) for p in range(n)]
    total = lax.dynamic_index_in_dim(parts, me, axis=0, keepdims=False)
    ahead = n // 2 if lead > 0 else n - 1 - n // 2
    for way, pairs, hops in ((1, forward, ahead), (-1, backward, n - 1 - ahead)):
        acc = None
        for step in range(hops):
            owner = order[(here + way * (hops - step)) % n]
            mine = lax.dynamic_index_in_dim(parts, owner, axis=0, keepdims=False)
            acc = lax.ppermute(mine if acc is None else acc + mine, "dp", pairs)
        total = total + acc
    return total

def ring_all_gather(piece, ring):
    n = len(ring)
    order = jnp.asarray(np.array(ring, np.int32))
    place = jnp.asarray(np.argsort(np.array(ring)).astype(np.int32))
    me = lax.axis_index("dp")
    here = place[me]
    forward = [(ring[p], ring[(p + 1) % n]) for p in range(n)]
    backward = [(ring[p], ring[(p - 1) % n]) for p in range(n)]
    held = lax.dynamic_update_index_in_dim(jnp.zeros((n,) + piece.shape, piece.dtype), piece, me, 0)
    ahead = n // 2
    for way, pairs, hops in ((1, forward, ahead), (-1, backward, n - 1 - ahead)):
        cur = piece
        for step in range(hops):
            cur = lax.ppermute(cur, "dp", pairs)
            owner = order[(here - way * (1 + step)) % n]
            held = lax.dynamic_update_index_in_dim(held, cur, owner, 0)
    return held

def body(ring, activations, cotangent, r_mix, l_mix):
    tok_count = activations.shape[1]
    local_blocks = activations.shape[0] // WIDTH
    n_dp = lax.axis_size("dp")
    grad_scale = 1.0 / math.sqrt(tok_count * n_dp)
    x_blocks = activations.reshape(local_blocks, WIDTH, tok_count)
    g_blocks = cotangent.reshape(local_blocks, WIDTH, tok_count)
    g_cols = lax.all_to_all(g_blocks, "feat", split_axis=1, concat_axis=0, tiled=True)
    local_cols = l_mix.shape[0]
    rows_r = r_mix.shape[1]
    r_lead = jnp.transpose(r_mix, (1, 0, 2)).reshape(-1, WIDTH)
    l_lead = jnp.transpose(l_mix.reshape(local_cols, -1, BLOCKS), (1, 0, 2)).reshape(-1, WIDTH)
    r_size = r_lead.shape[0]
    packed = jnp.concatenate([r_lead, l_lead], axis=0)
    packed = ring_all_gather(packed, ring)
    r_whole = packed[:, :r_size].reshape(n_dp * rows_r, local_blocks, WIDTH)
    l_blocks = packed[:, r_size:].reshape(-1, local_cols, BLOCKS)
    mixed_rows = jnp.einsum(
        "bit,ibo->bot", x_blocks, r_whole, preferred_element_type=jnp.float32
    ).astype(jnp.bfloat16)
    columns = lax.all_to_all(mixed_rows, "feat", split_axis=1, concat_axis=0, tiled=True)
    pre_act = jnp.einsum("bst,bsc->cst", columns, l_blocks, preferred_element_type=jnp.float32)
    slope_cols = slope_of(pre_act, g_cols)
    back_cols = jnp.einsum(
        "cst,bsc->sbt", slope_cols, l_blocks, preferred_element_type=jnp.float32
    ).astype(jnp.bfloat16)
    l_term = jnp.einsum("bst,cst->bsc", columns, slope_cols, preferred_element_type=jnp.float32)
    l_term = (l_term * grad_scale).reshape(n_dp, -1, local_cols, BLOCKS)
    grad_l = ring_reduce_scatter(l_term, ring, lead=-1)
    grad_l = jnp.transpose(grad_l, (1, 0, 2)).reshape(local_cols, -1)
    back_rows = lax.all_to_all(back_cols, "feat", split_axis=1, concat_axis=0, tiled=True)
    through_r = jnp.einsum("obt,ibo->bit", back_rows, r_whole, preferred_element_type=jnp.float32)
    grad_x = (
        (g_blocks.astype(jnp.float32) + through_r)
        .astype(jnp.bfloat16)
        .reshape(local_blocks * WIDTH, tok_count)
    )
    r_term = (
        jnp.einsum("bit,obt->ibo", x_blocks, back_rows, preferred_element_type=jnp.float32)
        * grad_scale
    ).reshape(n_dp, rows_r, local_blocks, WIDTH)
    cut = rows_r // 2
    grad_r = jnp.concatenate(
        [ring_reduce_scatter(r_term[:, :cut], ring), ring_reduce_scatter(r_term[:, cut:], ring, lead=-1)],
        axis=0,
    )
    grad_r = jnp.transpose(grad_r, (1, 0, 2))
    return (grad_x, grad_r, grad_l)


def solution(mesh):
    ring = ring_of(mesh)
    placed = (P("feat", "dp"), P("feat", "dp"), P("feat", "dp", None), P("feat", "dp"))
    return jax.shard_map(
        lambda *args: body(ring, *args),
        mesh=mesh,
        in_specs=placed,
        out_specs=(P("feat", "dp"), P("feat", "dp", None), P("feat", "dp")),
        check_vma=False,
    )
```

```python
import math

import jax
import jax.numpy as jnp
import numpy as np
from jax import lax
from jax.sharding import PartitionSpec as P

BLOCKS = 64
WIDTH = 256


def gelu_tanh(values):
    return jax.nn.gelu(values, approximate=True)


def slope_of(pre_act, upstream):
    _, pullback = jax.vjp(gelu_tanh, pre_act)
    return pullback(upstream.astype(jnp.float32))[0].astype(jnp.bfloat16)


def ring_of(mesh):
    row = mesh.devices[(slice(None),) + (0,) * (mesh.devices.ndim - 1)]
    size = len(row)
    try:
        spots = [tuple(d.coords) for d in row]
    except AttributeError:
        return list(range(size))
    near = [
        [j for j in range(size) if sum(abs(a - b) for a, b in zip(spots[i], spots[j])) == 1]
        for i in range(size)
    ]
    path, seen, budget = [0], {0}, [20000]

    def grow():
        budget[0] -= 1
        if budget[0] < 0:
            return False
        if len(path) == size:
            return 0 in near[path[-1]] or size <= 2
        here = path[-1]
        for nxt in sorted(near[here], key=lambda j: len([k for k in near[j] if k not in seen])):
            if nxt in seen:
                continue
            path.append(nxt)
            seen.add(nxt)
            if grow():
                return True
            path.pop()
            seen.discard(nxt)
        return False

    return list(path) if grow() else list(range(size))


def ring_reduce_scatter(parts, ring, lead=1):
    n = len(ring)
    order = jnp.asarray(np.array(ring, np.int32))
    place = jnp.asarray(np.argsort(np.array(ring)).astype(np.int32))
    me = lax.axis_index("dp")
    here = place[me]
    forward = [(ring[p], ring[(p + 1) % n]) for p in range(n)]
    backward = [(ring[p], ring[(p - 1) % n]) for p in range(n)]
    total = lax.dynamic_index_in_dim(parts, me, axis=0, keepdims=False)
    ahead = n // 2 if lead > 0 else n - 1 - n // 2
    for way, pairs, hops in ((1, forward, ahead), (-1, backward, n - 1 - ahead)):
        acc = None
        for step in range(hops):
            owner = order[(here + way * (hops - step)) % n]
            mine = lax.dynamic_index_in_dim(parts, owner, axis=0, keepdims=False)
            acc = lax.ppermute(mine if acc is None else acc + mine, "dp", pairs)
        total = total + acc
    return total

def ring_all_gather(piece, ring, lead=1):
    n = len(ring)
    order = jnp.asarray(np.array(ring, np.int32))
    place = jnp.asarray(np.argsort(np.array(ring)).astype(np.int32))
    me = lax.axis_index("dp")
    here = place[me]
    forward = [(ring[p], ring[(p + 1) % n]) for p in range(n)]
    backward = [(ring[p], ring[(p - 1) % n]) for p in range(n)]
    held = lax.dynamic_update_index_in_dim(jnp.zeros((n,) + piece.shape, piece.dtype), piece, me, 0)
    ahead = n // 2 if lead > 0 else n - 1 - n // 2
    for way, pairs, hops in ((1, forward, ahead), (-1, backward, n - 1 - ahead)):
        cur = piece
        for step in range(hops):
            cur = lax.ppermute(cur, "dp", pairs)
            owner = order[(here - way * (1 + step)) % n]
            held = lax.dynamic_update_index_in_dim(held, cur, owner, 0)
    return held

def body(ring, activations, cotangent, r_mix, l_mix):
    tok_count = activations.shape[1]
    local_blocks = activations.shape[0] // WIDTH
    n_dp = lax.axis_size("dp")
    grad_scale = 1.0 / math.sqrt(tok_count * n_dp)
    x_blocks = activations.reshape(local_blocks, WIDTH, tok_count)
    g_blocks = cotangent.reshape(local_blocks, WIDTH, tok_count)
    g_cols = lax.all_to_all(g_blocks, "feat", split_axis=1, concat_axis=0, tiled=True)
    local_cols = l_mix.shape[0]
    rows_r = r_mix.shape[1]
    r_lead = jnp.transpose(r_mix, (1, 0, 2)).reshape(-1, WIDTH)
    l_lead = jnp.transpose(l_mix.reshape(local_cols, -1, BLOCKS), (1, 0, 2)).reshape(-1, WIDTH)
    r_size = r_lead.shape[0]
    packed = jnp.concatenate([r_lead, l_lead], axis=0)
    split = packed.shape[0] // 2
    packed = jnp.concatenate(
        [ring_all_gather(packed[:split], ring), ring_all_gather(packed[split:], ring, lead=-1)], axis=1
    )
    r_whole = packed[:, :r_size].reshape(n_dp * rows_r, local_blocks, WIDTH)
    l_blocks = packed[:, r_size:].reshape(-1, local_cols, BLOCKS)
    mixed_rows = jnp.einsum(
        "bit,ibo->bot", x_blocks, r_whole, preferred_element_type=jnp.float32
    ).astype(jnp.bfloat16)
    columns = lax.all_to_all(mixed_rows, "feat", split_axis=1, concat_axis=0, tiled=True)
    pre_act = jnp.einsum("bst,bsc->cst", columns, l_blocks, preferred_element_type=jnp.float32)
    slope_cols = slope_of(pre_act, g_cols)
    back_cols = jnp.einsum(
        "cst,bsc->sbt", slope_cols, l_blocks, preferred_element_type=jnp.float32
    ).astype(jnp.bfloat16)
    l_term = jnp.einsum("bst,cst->bsc", columns, slope_cols, preferred_element_type=jnp.float32)
    l_term = (l_term * grad_scale).reshape(n_dp, -1, local_cols, BLOCKS)
    grad_l = ring_reduce_scatter(l_term, ring, lead=-1)
    grad_l = jnp.transpose(grad_l, (1, 0, 2)).reshape(local_cols, -1)
    back_rows = lax.all_to_all(back_cols, "feat", split_axis=1, concat_axis=0, tiled=True)
    through_r = jnp.einsum("obt,ibo->bit", back_rows, r_whole, preferred_element_type=jnp.float32)
    grad_x = (
        (g_blocks.astype(jnp.float32) + through_r)
        .astype(jnp.bfloat16)
        .reshape(local_blocks * WIDTH, tok_count)
    )
    r_term = (
        jnp.einsum("bit,obt->ibo", x_blocks, back_rows, preferred_element_type=jnp.float32)
        * grad_scale
    ).reshape(n_dp, rows_r, local_blocks, WIDTH)
    cut = rows_r // 2
    grad_r = jnp.concatenate(
        [ring_reduce_scatter(r_term[:, :cut], ring), ring_reduce_scatter(r_term[:, cut:], ring, lead=-1)],
        axis=0,
    )
    grad_r = jnp.transpose(grad_r, (1, 0, 2))
    return (grad_x, grad_r, grad_l)


def solution(mesh):
    ring = ring_of(mesh)
    placed = (P("feat", "dp"), P("feat", "dp"), P("feat", "dp", None), P("feat", "dp"))
    return jax.shard_map(
        lambda *args: body(ring, *args),
        mesh=mesh,
        in_specs=placed,
        out_specs=(P("feat", "dp"), P("feat", "dp", None), P("feat", "dp")),
        check_vma=False,
    )
```

```python
import math

import jax
import jax.numpy as jnp
import numpy as np
from jax import lax
from jax.sharding import PartitionSpec as P

BLOCKS = 64
WIDTH = 256


def gelu_tanh(values):
    return jax.nn.gelu(values, approximate=True)


def slope_of(pre_act, upstream):
    _, pullback = jax.vjp(gelu_tanh, pre_act)
    return pullback(upstream.astype(jnp.float32))[0].astype(jnp.bfloat16)


def ring_of(mesh):
    row = mesh.devices[(slice(None),) + (0,) * (mesh.devices.ndim - 1)]
    size = len(row)
    try:
        spots = [tuple(d.coords) for d in row]
    except AttributeError:
        return list(range(size))
    near = [
        [j for j in range(size) if sum(abs(a - b) for a, b in zip(spots[i], spots[j])) == 1]
        for i in range(size)
    ]
    path, seen, budget = [0], {0}, [20000]

    def grow():
        budget[0] -= 1
        if budget[0] < 0:
            return False
        if len(path) == size:
            return 0 in near[path[-1]] or size <= 2
        here = path[-1]
        for nxt in sorted(near[here], key=lambda j: len([k for k in near[j] if k not in seen])):
            if nxt in seen:
                continue
            path.append(nxt)
            seen.add(nxt)
            if grow():
                return True
            path.pop()
            seen.discard(nxt)
        return False

    return list(path) if grow() else list(range(size))


def ring_reduce_scatter(parts, ring, lead=1):
    n = len(ring)
    order = jnp.asarray(np.array(ring, np.int32))
    place = jnp.asarray(np.argsort(np.array(ring)).astype(np.int32))
    me = lax.axis_index("dp")
    here = place[me]
    forward = [(ring[p], ring[(p + 1) % n]) for p in range(n)]
    backward = [(ring[p], ring[(p - 1) % n]) for p in range(n)]
    total = lax.dynamic_index_in_dim(parts, me, axis=0, keepdims=False)
    ahead = n // 2 if lead > 0 else n - 1 - n // 2
    for way, pairs, hops in ((1, forward, ahead), (-1, backward, n - 1 - ahead)):
        acc = None
        for step in range(hops):
            owner = order[(here + way * (hops - step)) % n]
            mine = lax.dynamic_index_in_dim(parts, owner, axis=0, keepdims=False)
            acc = lax.ppermute(mine if acc is None else acc + mine, "dp", pairs)
        total = total + acc
    return total

def ring_all_gather(piece, ring):
    n = len(ring)
    order = jnp.asarray(np.array(ring, np.int32))
    place = jnp.asarray(np.argsort(np.array(ring)).astype(np.int32))
    me = lax.axis_index("dp")
    here = place[me]
    forward = [(ring[p], ring[(p + 1) % n]) for p in range(n)]
    backward = [(ring[p], ring[(p - 1) % n]) for p in range(n)]
    held = lax.dynamic_update_index_in_dim(jnp.zeros((n,) + piece.shape, piece.dtype), piece, me, 0)
    ahead = n // 2
    for way, pairs, hops in ((1, forward, ahead), (-1, backward, n - 1 - ahead)):
        cur = piece
        for step in range(hops):
            cur = lax.ppermute(cur, "dp", pairs)
            owner = order[(here - way * (1 + step)) % n]
            held = lax.dynamic_update_index_in_dim(held, cur, owner, 0)
    return held

def body(ring, activations, cotangent, r_mix, l_mix):
    tok_count = activations.shape[1]
    local_blocks = activations.shape[0] // WIDTH
    n_dp = lax.axis_size("dp")
    grad_scale = 1.0 / math.sqrt(tok_count * n_dp)
    x_blocks = activations.reshape(local_blocks, WIDTH, tok_count)
    g_blocks = cotangent.reshape(local_blocks, WIDTH, tok_count)
    g_cols = lax.all_to_all(g_blocks, "feat", split_axis=1, concat_axis=0, tiled=True)
    local_cols = l_mix.shape[0]
    rows_r = r_mix.shape[1]
    r_lead = jnp.transpose(r_mix, (1, 0, 2)).reshape(-1, WIDTH)
    l_lead = jnp.transpose(l_mix.reshape(local_cols, -1, BLOCKS), (1, 0, 2)).reshape(-1, WIDTH)
    r_size = r_lead.shape[0]
    packed = jnp.concatenate([r_lead, l_lead], axis=0)
    packed = ring_all_gather(packed, ring)
    r_whole = packed[:, :r_size].reshape(n_dp * rows_r, local_blocks, WIDTH)
    l_blocks = packed[:, r_size:].reshape(-1, local_cols, BLOCKS)
    mixed_rows = jnp.einsum(
        "bit,ibo->bot", x_blocks, r_whole, preferred_element_type=jnp.float32
    ).astype(jnp.bfloat16)
    columns = lax.all_to_all(mixed_rows, "feat", split_axis=1, concat_axis=0, tiled=True)
    pre_act = jnp.einsum("bst,bsc->cst", columns, l_blocks, preferred_element_type=jnp.float32)
    slope_cols = slope_of(pre_act, g_cols)
    back_cols = jnp.einsum(
        "cst,bsc->sbt", slope_cols, l_blocks, preferred_element_type=jnp.float32
    ).astype(jnp.bfloat16)
    l_term = jnp.einsum("bst,cst->bsc", columns, slope_cols, preferred_element_type=jnp.float32)
    l_term = (l_term * grad_scale).reshape(n_dp, -1, local_cols, BLOCKS)
    grad_l = ring_reduce_scatter(l_term, ring, lead=-1)
    grad_l = jnp.transpose(grad_l, (1, 0, 2)).reshape(local_cols, -1)
    back_rows = lax.all_to_all(back_cols, "feat", split_axis=1, concat_axis=0, tiled=True)
    through_r = jnp.einsum("obt,ibo->bit", back_rows, r_whole, preferred_element_type=jnp.float32)
    grad_x = (
        (g_blocks.astype(jnp.float32) + through_r)
        .astype(jnp.bfloat16)
        .reshape(local_blocks * WIDTH, tok_count)
    )
    r_term = (
        jnp.einsum("bit,obt->ibo", x_blocks, back_rows, preferred_element_type=jnp.float32)
        * grad_scale
    ).reshape(n_dp, rows_r, local_blocks, WIDTH)
    step = rows_r // 4
    grad_r = jnp.concatenate(
        [
            ring_reduce_scatter(r_term[:, k * step:(k + 1) * step], ring, lead=1 - 2 * (k % 2))
            for k in range(4)
        ],
        axis=0,
    )
    grad_r = jnp.transpose(grad_r, (1, 0, 2))
    return (grad_x, grad_r, grad_l)


def solution(mesh):
    ring = ring_of(mesh)
    placed = (P("feat", "dp"), P("feat", "dp"), P("feat", "dp", None), P("feat", "dp"))
    return jax.shard_map(
        lambda *args: body(ring, *args),
        mesh=mesh,
        in_specs=placed,
        out_specs=(P("feat", "dp"), P("feat", "dp", None), P("feat", "dp")),
        check_vma=False,
    )
```

```python
import math

import jax
import jax.numpy as jnp
import numpy as np
from jax import lax
from jax.sharding import PartitionSpec as P

BLOCKS = 64
WIDTH = 256


def gelu_tanh(values):
    return jax.nn.gelu(values, approximate=True)


def slope_of(pre_act, upstream):
    _, pullback = jax.vjp(gelu_tanh, pre_act)
    return pullback(upstream.astype(jnp.float32))[0].astype(jnp.bfloat16)


def ring_of(mesh):
    row = mesh.devices[(slice(None),) + (0,) * (mesh.devices.ndim - 1)]
    size = len(row)
    try:
        spots = [tuple(d.coords) for d in row]
    except AttributeError:
        return list(range(size))
    near = [
        [j for j in range(size) if sum(abs(a - b) for a, b in zip(spots[i], spots[j])) == 1]
        for i in range(size)
    ]
    path, seen, budget = [0], {0}, [20000]

    def grow():
        budget[0] -= 1
        if budget[0] < 0:
            return False
        if len(path) == size:
            return 0 in near[path[-1]] or size <= 2
        here = path[-1]
        for nxt in sorted(near[here], key=lambda j: len([k for k in near[j] if k not in seen])):
            if nxt in seen:
                continue
            path.append(nxt)
            seen.add(nxt)
            if grow():
                return True
            path.pop()
            seen.discard(nxt)
        return False

    return list(path) if grow() else list(range(size))


def ring_reduce_scatter(parts, ring, lead=1):
    n = len(ring)
    order = jnp.asarray(np.array(ring, np.int32))
    place = jnp.asarray(np.argsort(np.array(ring)).astype(np.int32))
    me = lax.axis_index("dp")
    here = place[me]
    forward = [(ring[p], ring[(p + 1) % n]) for p in range(n)]
    backward = [(ring[p], ring[(p - 1) % n]) for p in range(n)]
    total = lax.dynamic_index_in_dim(parts, me, axis=0, keepdims=False)
    ahead = n // 2 if lead > 0 else n - 1 - n // 2
    for way, pairs, hops in ((1, forward, ahead), (-1, backward, n - 1 - ahead)):
        acc = None
        for step in range(hops):
            owner = order[(here + way * (hops - step)) % n]
            mine = lax.dynamic_index_in_dim(parts, owner, axis=0, keepdims=False)
            acc = lax.ppermute(mine if acc is None else acc + mine, "dp", pairs)
        total = total + acc
    return total

def ring_all_gather(piece, ring):
    n = len(ring)
    order = jnp.asarray(np.array(ring, np.int32))
    place = jnp.asarray(np.argsort(np.array(ring)).astype(np.int32))
    me = lax.axis_index("dp")
    here = place[me]
    forward = [(ring[p], ring[(p + 1) % n]) for p in range(n)]
    backward = [(ring[p], ring[(p - 1) % n]) for p in range(n)]
    held = lax.dynamic_update_index_in_dim(jnp.zeros((n,) + piece.shape, piece.dtype), piece, me, 0)
    ahead = n // 2
    for way, pairs, hops in ((1, forward, ahead), (-1, backward, n - 1 - ahead)):
        cur = piece
        for step in range(hops):
            cur = lax.ppermute(cur, "dp", pairs)
            owner = order[(here - way * (1 + step)) % n]
            held = lax.dynamic_update_index_in_dim(held, cur, owner, 0)
    return held

def body(ring, activations, cotangent, r_mix, l_mix):
    tok_count = activations.shape[1]
    local_blocks = activations.shape[0] // WIDTH
    n_dp = lax.axis_size("dp")
    grad_scale = 1.0 / math.sqrt(tok_count * n_dp)
    x_blocks = activations.reshape(local_blocks, WIDTH, tok_count)
    g_blocks = cotangent.reshape(local_blocks, WIDTH, tok_count)
    g_cols = lax.all_to_all(g_blocks, "feat", split_axis=1, concat_axis=0, tiled=True)
    local_cols = l_mix.shape[0]
    rows_r = r_mix.shape[1]
    r_lead = jnp.transpose(r_mix, (1, 0, 2)).reshape(-1, WIDTH)
    l_lead = jnp.transpose(l_mix.reshape(local_cols, -1, BLOCKS), (1, 0, 2)).reshape(-1, WIDTH)
    r_size = r_lead.shape[0]
    packed = jnp.concatenate([r_lead, l_lead], axis=0)
    packed = ring_all_gather(packed, ring)
    r_whole = packed[:, :r_size].reshape(n_dp * rows_r, local_blocks, WIDTH)
    l_blocks = packed[:, r_size:].reshape(-1, local_cols, BLOCKS)
    mixed_rows = jnp.einsum(
        "bit,ibo->bot", x_blocks, r_whole, preferred_element_type=jnp.float32
    ).astype(jnp.bfloat16)
    columns = lax.all_to_all(mixed_rows, "feat", split_axis=1, concat_axis=0, tiled=True)
    pre_act = jnp.einsum("bst,bsc->cst", columns, l_blocks, preferred_element_type=jnp.float32)
    slope_cols = slope_of(pre_act, g_cols)
    back_cols = jnp.einsum(
        "cst,bsc->sbt", slope_cols, l_blocks, preferred_element_type=jnp.float32
    ).astype(jnp.bfloat16)
    l_term = jnp.einsum("bst,cst->bsc", columns, slope_cols, preferred_element_type=jnp.float32)
    l_term = (l_term * grad_scale).reshape(n_dp, -1, local_cols, BLOCKS)
    half_l = l_term.shape[1] // 2
    grad_l = jnp.concatenate(
        [ring_reduce_scatter(l_term[:, :half_l], ring), ring_reduce_scatter(l_term[:, half_l:], ring, lead=-1)],
        axis=0,
    )
    grad_l = jnp.transpose(grad_l, (1, 0, 2)).reshape(local_cols, -1)
    back_rows = lax.all_to_all(back_cols, "feat", split_axis=1, concat_axis=0, tiled=True)
    through_r = jnp.einsum("obt,ibo->bit", back_rows, r_whole, preferred_element_type=jnp.float32)
    grad_x = (
        (g_blocks.astype(jnp.float32) + through_r)
        .astype(jnp.bfloat16)
        .reshape(local_blocks * WIDTH, tok_count)
    )
    r_term = (
        jnp.einsum("bit,obt->ibo", x_blocks, back_rows, preferred_element_type=jnp.float32)
        * grad_scale
    ).reshape(n_dp, rows_r, local_blocks, WIDTH)
    cut = rows_r // 2
    grad_r = jnp.concatenate(
        [ring_reduce_scatter(r_term[:, :cut], ring), ring_reduce_scatter(r_term[:, cut:], ring, lead=-1)],
        axis=0,
    )
    grad_r = jnp.transpose(grad_r, (1, 0, 2))
    return (grad_x, grad_r, grad_l)


def solution(mesh):
    ring = ring_of(mesh)
    placed = (P("feat", "dp"), P("feat", "dp"), P("feat", "dp", None), P("feat", "dp"))
    return jax.shard_map(
        lambda *args: body(ring, *args),
        mesh=mesh,
        in_specs=placed,
        out_specs=(P("feat", "dp"), P("feat", "dp", None), P("feat", "dp")),
        check_vma=False,
    )
```

```python
import math

import jax
import jax.numpy as jnp
import numpy as np
from jax import lax
from jax.sharding import PartitionSpec as P

BLOCKS = 64
WIDTH = 256


def gelu_tanh(values):
    return jax.nn.gelu(values, approximate=True)


def slope_of(pre_act, upstream):
    _, pullback = jax.vjp(gelu_tanh, pre_act)
    return pullback(upstream.astype(jnp.float32))[0].astype(jnp.bfloat16)


def ring_of(mesh):
    row = mesh.devices[(slice(None),) + (0,) * (mesh.devices.ndim - 1)]
    size = len(row)
    try:
        spots = [tuple(d.coords) for d in row]
    except AttributeError:
        return list(range(size))
    near = [
        [j for j in range(size) if sum(abs(a - b) for a, b in zip(spots[i], spots[j])) == 1]
        for i in range(size)
    ]
    path, seen, budget = [0], {0}, [20000]

    def grow():
        budget[0] -= 1
        if budget[0] < 0:
            return False
        if len(path) == size:
            return 0 in near[path[-1]] or size <= 2
        here = path[-1]
        for nxt in sorted(near[here], key=lambda j: len([k for k in near[j] if k not in seen])):
            if nxt in seen:
                continue
            path.append(nxt)
            seen.add(nxt)
            if grow():
                return True
            path.pop()
            seen.discard(nxt)
        return False

    return list(path) if grow() else list(range(size))


def ring_reduce_scatter(parts, ring, lead=1):
    n = len(ring)
    order = jnp.asarray(np.array(ring, np.int32))
    place = jnp.asarray(np.argsort(np.array(ring)).astype(np.int32))
    me = lax.axis_index("dp")
    here = place[me]
    forward = [(ring[p], ring[(p + 1) % n]) for p in range(n)]
    backward = [(ring[p], ring[(p - 1) % n]) for p in range(n)]
    total = lax.dynamic_index_in_dim(parts, me, axis=0, keepdims=False)
    ahead = n // 2 if lead > 0 else n - 1 - n // 2
    for way, pairs, hops in ((1, forward, ahead), (-1, backward, n - 1 - ahead)):
        acc = None
        for step in range(hops):
            owner = order[(here + way * (hops - step)) % n]
            mine = lax.dynamic_index_in_dim(parts, owner, axis=0, keepdims=False)
            acc = lax.ppermute(mine if acc is None else acc + mine, "dp", pairs)
        total = total + acc
    return total

def ring_all_gather(piece, ring):
    n = len(ring)
    order = jnp.asarray(np.array(ring, np.int32))
    place = jnp.asarray(np.argsort(np.array(ring)).astype(np.int32))
    me = lax.axis_index("dp")
    here = place[me]
    forward = [(ring[p], ring[(p + 1) % n]) for p in range(n)]
    backward = [(ring[p], ring[(p - 1) % n]) for p in range(n)]
    held = lax.dynamic_update_index_in_dim(jnp.zeros((n,) + piece.shape, piece.dtype), piece, me, 0)
    ahead = n // 2
    for way, pairs, hops in ((1, forward, ahead), (-1, backward, n - 1 - ahead)):
        cur = piece
        for step in range(hops):
            cur = lax.ppermute(cur, "dp", pairs)
            owner = order[(here - way * (1 + step)) % n]
            held = lax.dynamic_update_index_in_dim(held, cur, owner, 0)
    return held

def permute_all_to_all(blocks, axis):
    n = lax.axis_size("feat")
    me = lax.axis_index("feat")
    pieces = jnp.stack(jnp.split(blocks, n, axis=axis))
    by_shift = [lax.dynamic_index_in_dim(pieces, me, axis=0, keepdims=False)]
    for shift in range(1, n):
        mine = lax.dynamic_index_in_dim(pieces, (me + shift) % n, axis=0, keepdims=False)
        by_shift.append(lax.ppermute(mine, "feat", [(f, (f + shift) % n) for f in range(n)]))
    by_shift = jnp.stack(by_shift)
    came = [lax.dynamic_index_in_dim(by_shift, (me - src) % n, axis=0, keepdims=False) for src in range(n)]
    return jnp.concatenate(came, axis=0)


def body(ring, activations, cotangent, r_mix, l_mix):
    tok_count = activations.shape[1]
    local_blocks = activations.shape[0] // WIDTH
    n_dp = lax.axis_size("dp")
    grad_scale = 1.0 / math.sqrt(tok_count * n_dp)
    x_blocks = activations.reshape(local_blocks, WIDTH, tok_count)
    g_blocks = cotangent.reshape(local_blocks, WIDTH, tok_count)
    g_cols = lax.all_to_all(g_blocks, "feat", split_axis=1, concat_axis=0, tiled=True)
    local_cols = l_mix.shape[0]
    rows_r = r_mix.shape[1]
    r_lead = jnp.transpose(r_mix, (1, 0, 2)).reshape(-1, WIDTH)
    l_lead = jnp.transpose(l_mix.reshape(local_cols, -1, BLOCKS), (1, 0, 2)).reshape(-1, WIDTH)
    r_size = r_lead.shape[0]
    packed = jnp.concatenate([r_lead, l_lead], axis=0)
    packed = ring_all_gather(packed, ring)
    r_whole = packed[:, :r_size].reshape(n_dp * rows_r, local_blocks, WIDTH)
    l_blocks = packed[:, r_size:].reshape(-1, local_cols, BLOCKS)
    mixed_rows = jnp.einsum(
        "bit,ibo->bot", x_blocks, r_whole, preferred_element_type=jnp.float32
    ).astype(jnp.bfloat16)
    columns = permute_all_to_all(mixed_rows, 1)
    pre_act = jnp.einsum("bst,bsc->cst", columns, l_blocks, preferred_element_type=jnp.float32)
    slope_cols = slope_of(pre_act, g_cols)
    back_cols = jnp.einsum(
        "cst,bsc->sbt", slope_cols, l_blocks, preferred_element_type=jnp.float32
    ).astype(jnp.bfloat16)
    l_term = jnp.einsum("bst,cst->bsc", columns, slope_cols, preferred_element_type=jnp.float32)
    l_term = (l_term * grad_scale).reshape(n_dp, -1, local_cols, BLOCKS)
    grad_l = ring_reduce_scatter(l_term, ring, lead=-1)
    grad_l = jnp.transpose(grad_l, (1, 0, 2)).reshape(local_cols, -1)
    back_rows = lax.all_to_all(back_cols, "feat", split_axis=1, concat_axis=0, tiled=True)
    through_r = jnp.einsum("obt,ibo->bit", back_rows, r_whole, preferred_element_type=jnp.float32)
    grad_x = (
        (g_blocks.astype(jnp.float32) + through_r)
        .astype(jnp.bfloat16)
        .reshape(local_blocks * WIDTH, tok_count)
    )
    r_term = (
        jnp.einsum("bit,obt->ibo", x_blocks, back_rows, preferred_element_type=jnp.float32)
        * grad_scale
    ).reshape(n_dp, rows_r, local_blocks, WIDTH)
    cut = rows_r // 2
    grad_r = jnp.concatenate(
        [ring_reduce_scatter(r_term[:, :cut], ring), ring_reduce_scatter(r_term[:, cut:], ring, lead=-1)],
        axis=0,
    )
    grad_r = jnp.transpose(grad_r, (1, 0, 2))
    return (grad_x, grad_r, grad_l)


def solution(mesh):
    ring = ring_of(mesh)
    placed = (P("feat", "dp"), P("feat", "dp"), P("feat", "dp", None), P("feat", "dp"))
    return jax.shard_map(
        lambda *args: body(ring, *args),
        mesh=mesh,
        in_specs=placed,
        out_specs=(P("feat", "dp"), P("feat", "dp", None), P("feat", "dp")),
        check_vma=False,
    )
```

```python
import math

import jax
import jax.numpy as jnp
import numpy as np
from jax import lax
from jax.sharding import PartitionSpec as P

BLOCKS = 64
WIDTH = 256


def gelu_tanh(values):
    return jax.nn.gelu(values, approximate=True)


def slope_of(pre_act, upstream):
    _, pullback = jax.vjp(gelu_tanh, pre_act)
    return pullback(upstream.astype(jnp.float32))[0].astype(jnp.bfloat16)


def ring_of(mesh):
    row = mesh.devices[(slice(None),) + (0,) * (mesh.devices.ndim - 1)]
    size = len(row)
    try:
        spots = [tuple(d.coords) for d in row]
    except AttributeError:
        return list(range(size))
    near = [
        [j for j in range(size) if sum(abs(a - b) for a, b in zip(spots[i], spots[j])) == 1]
        for i in range(size)
    ]
    path, seen, budget = [0], {0}, [20000]

    def grow():
        budget[0] -= 1
        if budget[0] < 0:
            return False
        if len(path) == size:
            return 0 in near[path[-1]] or size <= 2
        here = path[-1]
        for nxt in sorted(near[here], key=lambda j: len([k for k in near[j] if k not in seen])):
            if nxt in seen:
                continue
            path.append(nxt)
            seen.add(nxt)
            if grow():
                return True
            path.pop()
            seen.discard(nxt)
        return False

    return list(path) if grow() else list(range(size))


def ring_reduce_scatter(parts, ring, lead=1):
    n = len(ring)
    order = jnp.asarray(np.array(ring, np.int32))
    place = jnp.asarray(np.argsort(np.array(ring)).astype(np.int32))
    me = lax.axis_index("dp")
    here = place[me]
    forward = [(ring[p], ring[(p + 1) % n]) for p in range(n)]
    backward = [(ring[p], ring[(p - 1) % n]) for p in range(n)]
    total = lax.dynamic_index_in_dim(parts, me, axis=0, keepdims=False)
    ahead = n // 2 if lead > 0 else n - 1 - n // 2
    for way, pairs, hops in ((1, forward, ahead), (-1, backward, n - 1 - ahead)):
        acc = None
        for step in range(hops):
            owner = order[(here + way * (hops - step)) % n]
            mine = lax.dynamic_index_in_dim(parts, owner, axis=0, keepdims=False)
            acc = lax.ppermute(mine if acc is None else acc + mine, "dp", pairs)
        total = total + acc
    return total

def ring_all_gather(piece, ring):
    n = len(ring)
    order = jnp.asarray(np.array(ring, np.int32))
    place = jnp.asarray(np.argsort(np.array(ring)).astype(np.int32))
    me = lax.axis_index("dp")
    here = place[me]
    forward = [(ring[p], ring[(p + 1) % n]) for p in range(n)]
    backward = [(ring[p], ring[(p - 1) % n]) for p in range(n)]
    held = lax.dynamic_update_index_in_dim(jnp.zeros((n,) + piece.shape, piece.dtype), piece, me, 0)
    ahead = n // 2
    for way, pairs, hops in ((1, forward, ahead), (-1, backward, n - 1 - ahead)):
        cur = piece
        for step in range(hops):
            cur = lax.ppermute(cur, "dp", pairs)
            owner = order[(here - way * (1 + step)) % n]
            held = lax.dynamic_update_index_in_dim(held, cur, owner, 0)
    return held

def permute_all_to_all(blocks, axis):
    n = lax.axis_size("feat")
    me = lax.axis_index("feat")
    pieces = jnp.stack(jnp.split(blocks, n, axis=axis))
    by_shift = [lax.dynamic_index_in_dim(pieces, me, axis=0, keepdims=False)]
    for shift in range(1, n):
        mine = lax.dynamic_index_in_dim(pieces, (me + shift) % n, axis=0, keepdims=False)
        by_shift.append(lax.ppermute(mine, "feat", [(f, (f + shift) % n) for f in range(n)]))
    by_shift = jnp.stack(by_shift)
    came = [lax.dynamic_index_in_dim(by_shift, (me - src) % n, axis=0, keepdims=False) for src in range(n)]
    return jnp.concatenate(came, axis=0)


def body(ring, activations, cotangent, r_mix, l_mix):
    tok_count = activations.shape[1]
    local_blocks = activations.shape[0] // WIDTH
    n_dp = lax.axis_size("dp")
    grad_scale = 1.0 / math.sqrt(tok_count * n_dp)
    x_blocks = activations.reshape(local_blocks, WIDTH, tok_count)
    g_blocks = cotangent.reshape(local_blocks, WIDTH, tok_count)
    g_cols = lax.all_to_all(g_blocks, "feat", split_axis=1, concat_axis=0, tiled=True)
    local_cols = l_mix.shape[0]
    rows_r = r_mix.shape[1]
    r_lead = jnp.transpose(r_mix, (1, 0, 2)).reshape(-1, WIDTH)
    l_lead = jnp.transpose(l_mix.reshape(local_cols, -1, BLOCKS), (1, 0, 2)).reshape(-1, WIDTH)
    r_size = r_lead.shape[0]
    packed = jnp.concatenate([r_lead, l_lead], axis=0)
    packed = ring_all_gather(packed, ring)
    r_whole = packed[:, :r_size].reshape(n_dp * rows_r, local_blocks, WIDTH)
    l_blocks = packed[:, r_size:].reshape(-1, local_cols, BLOCKS)
    mixed_rows = jnp.einsum(
        "bit,ibo->bot", x_blocks, r_whole, preferred_element_type=jnp.float32
    ).astype(jnp.bfloat16)
    columns = permute_all_to_all(mixed_rows, 1)
    pre_act = jnp.einsum("bst,bsc->cst", columns, l_blocks, preferred_element_type=jnp.float32)
    slope_cols = slope_of(pre_act, g_cols)
    back_cols = jnp.einsum(
        "cst,bsc->sbt", slope_cols, l_blocks, preferred_element_type=jnp.float32
    ).astype(jnp.bfloat16)
    l_term = jnp.einsum("bst,cst->bsc", columns, slope_cols, preferred_element_type=jnp.float32)
    l_term = (l_term * grad_scale).reshape(n_dp, -1, local_cols, BLOCKS)
    grad_l = ring_reduce_scatter(l_term, ring, lead=-1)
    grad_l = jnp.transpose(grad_l, (1, 0, 2)).reshape(local_cols, -1)
    back_rows = permute_all_to_all(back_cols, 1)
    through_r = jnp.einsum("obt,ibo->bit", back_rows, r_whole, preferred_element_type=jnp.float32)
    grad_x = (
        (g_blocks.astype(jnp.float32) + through_r)
        .astype(jnp.bfloat16)
        .reshape(local_blocks * WIDTH, tok_count)
    )
    r_term = (
        jnp.einsum("bit,obt->ibo", x_blocks, back_rows, preferred_element_type=jnp.float32)
        * grad_scale
    ).reshape(n_dp, rows_r, local_blocks, WIDTH)
    cut = rows_r // 2
    grad_r = jnp.concatenate(
        [ring_reduce_scatter(r_term[:, :cut], ring), ring_reduce_scatter(r_term[:, cut:], ring, lead=-1)],
        axis=0,
    )
    grad_r = jnp.transpose(grad_r, (1, 0, 2))
    return (grad_x, grad_r, grad_l)


def solution(mesh):
    ring = ring_of(mesh)
    placed = (P("feat", "dp"), P("feat", "dp"), P("feat", "dp", None), P("feat", "dp"))
    return jax.shard_map(
        lambda *args: body(ring, *args),
        mesh=mesh,
        in_specs=placed,
        out_specs=(P("feat", "dp"), P("feat", "dp", None), P("feat", "dp")),
        check_vma=False,
    )
```

```python
import math

import jax
import jax.numpy as jnp
import numpy as np
from jax import lax
from jax.sharding import PartitionSpec as P

BLOCKS = 64
WIDTH = 256


def gelu_tanh(values):
    return jax.nn.gelu(values, approximate=True)


def slope_of(pre_act, upstream):
    _, pullback = jax.vjp(gelu_tanh, pre_act)
    return pullback(upstream.astype(jnp.float32))[0].astype(jnp.bfloat16)


def ring_of(mesh):
    row = mesh.devices[(slice(None),) + (0,) * (mesh.devices.ndim - 1)]
    size = len(row)
    try:
        spots = [tuple(d.coords) for d in row]
    except AttributeError:
        return list(range(size))
    near = [
        [j for j in range(size) if sum(abs(a - b) for a, b in zip(spots[i], spots[j])) == 1]
        for i in range(size)
    ]
    path, seen, budget = [0], {0}, [20000]

    def grow():
        budget[0] -= 1
        if budget[0] < 0:
            return False
        if len(path) == size:
            return 0 in near[path[-1]] or size <= 2
        here = path[-1]
        for nxt in sorted(near[here], key=lambda j: len([k for k in near[j] if k not in seen])):
            if nxt in seen:
                continue
            path.append(nxt)
            seen.add(nxt)
            if grow():
                return True
            path.pop()
            seen.discard(nxt)
        return False

    return list(path) if grow() else list(range(size))


def ring_reduce_scatter(parts, ring, lead=1):
    n = len(ring)
    order = jnp.asarray(np.array(ring, np.int32))
    place = jnp.asarray(np.argsort(np.array(ring)).astype(np.int32))
    me = lax.axis_index("dp")
    here = place[me]
    forward = [(ring[p], ring[(p + 1) % n]) for p in range(n)]
    backward = [(ring[p], ring[(p - 1) % n]) for p in range(n)]
    total = lax.dynamic_index_in_dim(parts, me, axis=0, keepdims=False)
    ahead = n // 2 if lead > 0 else n - 1 - n // 2
    for way, pairs, hops in ((1, forward, ahead), (-1, backward, n - 1 - ahead)):
        acc = None
        for step in range(hops):
            owner = order[(here + way * (hops - step)) % n]
            mine = lax.dynamic_index_in_dim(parts, owner, axis=0, keepdims=False)
            acc = lax.ppermute(mine if acc is None else acc + mine, "dp", pairs)
        total = total + acc
    return total

def ring_all_gather(piece, ring):
    n = len(ring)
    order = jnp.asarray(np.array(ring, np.int32))
    place = jnp.asarray(np.argsort(np.array(ring)).astype(np.int32))
    me = lax.axis_index("dp")
    here = place[me]
    forward = [(ring[p], ring[(p + 1) % n]) for p in range(n)]
    backward = [(ring[p], ring[(p - 1) % n]) for p in range(n)]
    held = lax.dynamic_update_index_in_dim(jnp.zeros((n,) + piece.shape, piece.dtype), piece, me, 0)
    ahead = n // 2
    for way, pairs, hops in ((1, forward, ahead), (-1, backward, n - 1 - ahead)):
        cur = piece
        for step in range(hops):
            cur = lax.ppermute(cur, "dp", pairs)
            owner = order[(here - way * (1 + step)) % n]
            held = lax.dynamic_update_index_in_dim(held, cur, owner, 0)
    return held

def permute_all_to_all(blocks, axis):
    n = lax.axis_size("feat")
    me = lax.axis_index("feat")
    pieces = jnp.stack(jnp.split(blocks, n, axis=axis))
    by_shift = [lax.dynamic_index_in_dim(pieces, me, axis=0, keepdims=False)]
    for shift in range(1, n):
        mine = lax.dynamic_index_in_dim(pieces, (me + shift) % n, axis=0, keepdims=False)
        by_shift.append(lax.ppermute(mine, "feat", [(f, (f + shift) % n) for f in range(n)]))
    by_shift = jnp.stack(by_shift)
    came = [lax.dynamic_index_in_dim(by_shift, (me - src) % n, axis=0, keepdims=False) for src in range(n)]
    return jnp.concatenate(came, axis=0)


def body(ring, activations, cotangent, r_mix, l_mix):
    tok_count = activations.shape[1]
    local_blocks = activations.shape[0] // WIDTH
    n_dp = lax.axis_size("dp")
    grad_scale = 1.0 / math.sqrt(tok_count * n_dp)
    x_blocks = activations.reshape(local_blocks, WIDTH, tok_count)
    g_blocks = cotangent.reshape(local_blocks, WIDTH, tok_count)
    g_cols = permute_all_to_all(g_blocks, 1)
    local_cols = l_mix.shape[0]
    rows_r = r_mix.shape[1]
    r_lead = jnp.transpose(r_mix, (1, 0, 2)).reshape(-1, WIDTH)
    l_lead = jnp.transpose(l_mix.reshape(local_cols, -1, BLOCKS), (1, 0, 2)).reshape(-1, WIDTH)
    r_size = r_lead.shape[0]
    packed = jnp.concatenate([r_lead, l_lead], axis=0)
    packed = ring_all_gather(packed, ring)
    r_whole = packed[:, :r_size].reshape(n_dp * rows_r, local_blocks, WIDTH)
    l_blocks = packed[:, r_size:].reshape(-1, local_cols, BLOCKS)
    mixed_rows = jnp.einsum(
        "bit,ibo->bot", x_blocks, r_whole, preferred_element_type=jnp.float32
    ).astype(jnp.bfloat16)
    columns = permute_all_to_all(mixed_rows, 1)
    pre_act = jnp.einsum("bst,bsc->cst", columns, l_blocks, preferred_element_type=jnp.float32)
    slope_cols = slope_of(pre_act, g_cols)
    back_cols = jnp.einsum(
        "cst,bsc->sbt", slope_cols, l_blocks, preferred_element_type=jnp.float32
    ).astype(jnp.bfloat16)
    l_term = jnp.einsum("bst,cst->bsc", columns, slope_cols, preferred_element_type=jnp.float32)
    l_term = (l_term * grad_scale).reshape(n_dp, -1, local_cols, BLOCKS)
    grad_l = ring_reduce_scatter(l_term, ring, lead=-1)
    grad_l = jnp.transpose(grad_l, (1, 0, 2)).reshape(local_cols, -1)
    back_rows = permute_all_to_all(back_cols, 1)
    through_r = jnp.einsum("obt,ibo->bit", back_rows, r_whole, preferred_element_type=jnp.float32)
    grad_x = (
        (g_blocks.astype(jnp.float32) + through_r)
        .astype(jnp.bfloat16)
        .reshape(local_blocks * WIDTH, tok_count)
    )
    r_term = (
        jnp.einsum("bit,obt->ibo", x_blocks, back_rows, preferred_element_type=jnp.float32)
        * grad_scale
    ).reshape(n_dp, rows_r, local_blocks, WIDTH)
    cut = rows_r // 2
    grad_r = jnp.concatenate(
        [ring_reduce_scatter(r_term[:, :cut], ring), ring_reduce_scatter(r_term[:, cut:], ring, lead=-1)],
        axis=0,
    )
    grad_r = jnp.transpose(grad_r, (1, 0, 2))
    return (grad_x, grad_r, grad_l)


def solution(mesh):
    ring = ring_of(mesh)
    placed = (P("feat", "dp"), P("feat", "dp"), P("feat", "dp", None), P("feat", "dp"))
    return jax.shard_map(
        lambda *args: body(ring, *args),
        mesh=mesh,
        in_specs=placed,
        out_specs=(P("feat", "dp"), P("feat", "dp", None), P("feat", "dp")),
        check_vma=False,
    )
```

```python
import math

import jax
import jax.numpy as jnp
import numpy as np
from jax import lax
from jax.sharding import PartitionSpec as P

BLOCKS = 64
WIDTH = 256


def gelu_tanh(values):
    return jax.nn.gelu(values, approximate=True)


def slope_of(pre_act, upstream):
    _, pullback = jax.vjp(gelu_tanh, pre_act)
    return pullback(upstream.astype(jnp.float32))[0].astype(jnp.bfloat16)


def ring_of(mesh):
    row = mesh.devices[(slice(None),) + (0,) * (mesh.devices.ndim - 1)]
    size = len(row)
    try:
        spots = [tuple(d.coords) for d in row]
    except AttributeError:
        return list(range(size))
    near = [
        [j for j in range(size) if sum(abs(a - b) for a, b in zip(spots[i], spots[j])) == 1]
        for i in range(size)
    ]
    path, seen, budget = [0], {0}, [20000]

    def grow():
        budget[0] -= 1
        if budget[0] < 0:
            return False
        if len(path) == size:
            return 0 in near[path[-1]] or size <= 2
        here = path[-1]
        for nxt in sorted(near[here], key=lambda j: len([k for k in near[j] if k not in seen])):
            if nxt in seen:
                continue
            path.append(nxt)
            seen.add(nxt)
            if grow():
                return True
            path.pop()
            seen.discard(nxt)
        return False

    return list(path) if grow() else list(range(size))


def ring_reduce_scatter(parts, ring, lead=1):
    n = len(ring)
    order = jnp.asarray(np.array(ring, np.int32))
    place = jnp.asarray(np.argsort(np.array(ring)).astype(np.int32))
    me = lax.axis_index("dp")
    here = place[me]
    forward = [(ring[p], ring[(p + 1) % n]) for p in range(n)]
    backward = [(ring[p], ring[(p - 1) % n]) for p in range(n)]
    total = lax.dynamic_index_in_dim(parts, me, axis=0, keepdims=False)
    ahead = n // 2 if lead > 0 else n - 1 - n // 2
    for way, pairs, hops in ((1, forward, ahead), (-1, backward, n - 1 - ahead)):
        acc = None
        for step in range(hops):
            owner = order[(here + way * (hops - step)) % n]
            mine = lax.dynamic_index_in_dim(parts, owner, axis=0, keepdims=False)
            acc = lax.ppermute(mine if acc is None else acc + mine, "dp", pairs)
        total = total + acc
    return total

def ring_all_gather(piece, ring, lead=1):
    n = len(ring)
    order = jnp.asarray(np.array(ring, np.int32))
    place = jnp.asarray(np.argsort(np.array(ring)).astype(np.int32))
    me = lax.axis_index("dp")
    here = place[me]
    forward = [(ring[p], ring[(p + 1) % n]) for p in range(n)]
    backward = [(ring[p], ring[(p - 1) % n]) for p in range(n)]
    held = lax.dynamic_update_index_in_dim(jnp.zeros((n,) + piece.shape, piece.dtype), piece, me, 0)
    ahead = n // 2 if lead > 0 else n - 1 - n // 2
    for way, pairs, hops in ((1, forward, ahead), (-1, backward, n - 1 - ahead)):
        cur = piece
        for step in range(hops):
            cur = lax.ppermute(cur, "dp", pairs)
            owner = order[(here - way * (1 + step)) % n]
            held = lax.dynamic_update_index_in_dim(held, cur, owner, 0)
    return held

def permute_all_to_all(blocks, axis):
    n = lax.axis_size("feat")
    me = lax.axis_index("feat")
    pieces = jnp.stack(jnp.split(blocks, n, axis=axis))
    by_shift = [lax.dynamic_index_in_dim(pieces, me, axis=0, keepdims=False)]
    for shift in range(1, n):
        mine = lax.dynamic_index_in_dim(pieces, (me + shift) % n, axis=0, keepdims=False)
        by_shift.append(lax.ppermute(mine, "feat", [(f, (f + shift) % n) for f in range(n)]))
    by_shift = jnp.stack(by_shift)
    came = [lax.dynamic_index_in_dim(by_shift, (me - src) % n, axis=0, keepdims=False) for src in range(n)]
    return jnp.concatenate(came, axis=0)


def body(ring, activations, cotangent, r_mix, l_mix):
    tok_count = activations.shape[1]
    local_blocks = activations.shape[0] // WIDTH
    n_dp = lax.axis_size("dp")
    grad_scale = 1.0 / math.sqrt(tok_count * n_dp)
    x_blocks = activations.reshape(local_blocks, WIDTH, tok_count)
    g_blocks = cotangent.reshape(local_blocks, WIDTH, tok_count)
    g_cols = permute_all_to_all(g_blocks, 1)
    local_cols = l_mix.shape[0]
    rows_r = r_mix.shape[1]
    r_lead = jnp.transpose(r_mix, (1, 0, 2)).reshape(-1, WIDTH)
    l_lead = jnp.transpose(l_mix.reshape(local_cols, -1, BLOCKS), (1, 0, 2)).reshape(-1, WIDTH)
    r_size = r_lead.shape[0]
    packed = jnp.concatenate([r_lead, l_lead], axis=0)
    split = packed.shape[0] // 2
    packed = jnp.concatenate(
        [ring_all_gather(packed[:split], ring), ring_all_gather(packed[split:], ring, lead=-1)], axis=1
    )
    r_whole = packed[:, :r_size].reshape(n_dp * rows_r, local_blocks, WIDTH)
    l_blocks = packed[:, r_size:].reshape(-1, local_cols, BLOCKS)
    mixed_rows = jnp.einsum(
        "bit,ibo->bot", x_blocks, r_whole, preferred_element_type=jnp.float32
    ).astype(jnp.bfloat16)
    columns = permute_all_to_all(mixed_rows, 1)
    pre_act = jnp.einsum("bst,bsc->cst", columns, l_blocks, preferred_element_type=jnp.float32)
    slope_cols = slope_of(pre_act, g_cols)
    back_cols = jnp.einsum(
        "cst,bsc->sbt", slope_cols, l_blocks, preferred_element_type=jnp.float32
    ).astype(jnp.bfloat16)
    l_term = jnp.einsum("bst,cst->bsc", columns, slope_cols, preferred_element_type=jnp.float32)
    l_term = (l_term * grad_scale).reshape(n_dp, -1, local_cols, BLOCKS)
    grad_l = ring_reduce_scatter(l_term, ring, lead=-1)
    grad_l = jnp.transpose(grad_l, (1, 0, 2)).reshape(local_cols, -1)
    back_rows = permute_all_to_all(back_cols, 1)
    through_r = jnp.einsum("obt,ibo->bit", back_rows, r_whole, preferred_element_type=jnp.float32)
    grad_x = (
        (g_blocks.astype(jnp.float32) + through_r)
        .astype(jnp.bfloat16)
        .reshape(local_blocks * WIDTH, tok_count)
    )
    r_term = (
        jnp.einsum("bit,obt->ibo", x_blocks, back_rows, preferred_element_type=jnp.float32)
        * grad_scale
    ).reshape(n_dp, rows_r, local_blocks, WIDTH)
    cut = rows_r // 2
    grad_r = jnp.concatenate(
        [ring_reduce_scatter(r_term[:, :cut], ring), ring_reduce_scatter(r_term[:, cut:], ring, lead=-1)],
        axis=0,
    )
    grad_r = jnp.transpose(grad_r, (1, 0, 2))
    return (grad_x, grad_r, grad_l)


def solution(mesh):
    ring = ring_of(mesh)
    placed = (P("feat", "dp"), P("feat", "dp"), P("feat", "dp", None), P("feat", "dp"))
    return jax.shard_map(
        lambda *args: body(ring, *args),
        mesh=mesh,
        in_specs=placed,
        out_specs=(P("feat", "dp"), P("feat", "dp", None), P("feat", "dp")),
        check_vma=False,
    )
```
